32 devices in a mesh: segment: 4 (over z), ctx: 4 (over y, x), head: 2 (over core).
Axes of the slice: x: 2, y: 2, z: 4, core: 2. Of those that a mesh axis runs over, the one named last changes fastest.
Arguments:
- inputs: bfloat16 [4, 512, 5120], P('segment', 'ctx'), may hold values from -6 to 6
- query: bfloat16 [4, 512, 20, 128], P('segment', 'ctx', 'head'), may hold values from -32 to 32
- grad_out: bfloat16 [4, 512, 20, 128], P('segment', 'ctx', 'head'), may hold values from -6 to 6
- w_key: bfloat16 [4, 5120, 512], P('segment', None, 'head'), may hold values from -0.078125 to 0.078125
- w_value: bfloat16 [4, 5120, 512], P('segment', None, 'head'), may hold values from -0.078125 to 0.078125
- keep_mask: int32 [512], replicated, may hold values from 0 to 1
Outputs:
- grad_input: float32 [4, 512, 5120], P('segment', 'ctx', 'head')
The draws below stay inside these ranges and needn't reach their ends.
All inputs are finite; a program needn't handle non-finite values.
Results may differ from the reference program's by a relative error of at most 0.022.
The reference program's roundings to bfloat16 on the way (of `probs_b` and `dscore_b`) count: a program that leaves them out, or rounds other values in their place, can miss the bound.
Values may be sent and summed in bfloat16 or wider, within the bound.
No kernel may reach another device: no remote copies, remote signals or barrier semaphores. Data moves between devices by JAX's collectives and lax.ppermute only.
A program may use at most 192 MiB of HBM per device.

```python
import math
import jax
import jax.numpy as jnp
from jax import lax

D = 5120
HEADS = 20
KV_HEADS = 4
HEAD_DIM = 128
SEQ = 512
SEGMENTS = 4


def draw_query(key, part):
    first = jax.random.fold_in(key, 0)
    base = jax.random.normal(first, (SEGMENTS, SEQ, HEADS, HEAD_DIM), jnp.float32)
    return jnp.clip(base, -32.0, 32.0).astype(jnp.bfloat16)


def place_ends(result, rng, least, largest):
    longest = result.shape.index(max(result.shape))
    spots = []
    for shift in (0, 1):
        where = [jax.random.randint(jax.random.fold_in(rng, axis), (), 0, length) for axis, length in enumerate(result.shape)]
        where[longest] = (where[longest] + shift) % result.shape[longest]
        spots.append(tuple(where))
    return result.at[spots[0]].set(least).at[spots[1]].set(largest)


def level_of(stream_key, dims, pieces, low, top_value):
    level = 1.0
    for dim, blocks in pieces:
        steps = jax.random.uniform(jax.random.fold_in(jax.random.fold_in(stream_key, 6), dim), (blocks,), jnp.float32, low / len(pieces), top_value / len(pieces))
        level = level * jnp.repeat(jnp.exp(steps), dims[dim] // blocks).reshape((-1,) + (1,) * (len(dims) - 1 - dim))
    return level


def bell_draw(key, shape, deviation, bound, shards=(), kind=jnp.bfloat16):
    values = jax.random.normal(key, shape, jnp.float32) * deviation
    if len(shards) > 0:
        values = level_of(key, shape, shards, -0.22, 0.18) * values
    return jnp.clip(values, min=-bound, max=bound).astype(kind)


def setup_inputs(seed: int = 0) -> dict:
    splits = jax.random.split(jax.random.key(seed), 7)
    return {
        "inputs": bell_draw(splits[0], (SEGMENTS, SEQ, D), 1.0, 6.0, ((0, 4), (1, 4))),
        "query": draw_query(jax.random.fold_in(splits[6], 71), 0),
        "grad_out": bell_draw(splits[2], (SEGMENTS, SEQ, HEADS, HEAD_DIM), 1.0, 6.0, ((0, 4), (1, 4), (2, 2))),
        "w_key": bell_draw(splits[3], (SEGMENTS, D, KV_HEADS * HEAD_DIM), D ** -0.5, 0.078125, ((0, 4), (2, 2))),
        "w_value": bell_draw(splits[4], (SEGMENTS, D, KV_HEADS * HEAD_DIM), D ** -0.5, 0.078125, ((0, 4), (2, 2))),
        "keep_mask": place_ends(jax.random.randint(splits[5], (SEQ,), 0, 2), jax.random.fold_in(splits[5], 1), 0, 1).astype(jnp.int32),
    }


def one_section(xs, query_s, grad_s, wk, wv, keep_mask):
    seq_rows = xs.shape[0]
    group_size = HEADS // KV_HEADS
    scaling = 1.0 / math.sqrt(HEAD_DIM)
    key_rows = jnp.dot(xs, wk, preferred_element_type=jnp.float32).astype(jnp.bfloat16)
    value_rows = jnp.dot(xs, wv, preferred_element_type=jnp.float32).astype(jnp.bfloat16)
    key_heads = key_rows.reshape(seq_rows, KV_HEADS, HEAD_DIM).astype(jnp.float32)
    value_heads = value_rows.reshape(seq_rows, KV_HEADS, HEAD_DIM).astype(jnp.float32)
    query_heads = query_s.reshape(seq_rows, KV_HEADS, group_size, HEAD_DIM).astype(jnp.float32)
    grad_heads = grad_s.reshape(seq_rows, KV_HEADS, group_size, HEAD_DIM).astype(jnp.float32)
    scores = jnp.einsum('tkgd,skd->kgts', query_heads, key_heads) * scaling
    row_pos = jnp.arange(seq_rows, dtype=jnp.int32)[:, None]
    col_pos = jnp.arange(seq_rows, dtype=jnp.int32)[None, :]
    allowed = (col_pos <= row_pos) & ((keep_mask[None, :] == 1) | (col_pos == row_pos))
    masked = jnp.where(allowed, scores, -1e+30)
    top_score = lax.optimization_barrier(jnp.max(masked, axis=-1, keepdims=True))
    totals = lax.optimization_barrier(jnp.sum(jnp.where(allowed, jnp.exp(masked - top_score), 0.0), axis=-1, keepdims=True))
    log_total = top_score + jnp.log(totals)
    prob_full = jnp.where(allowed, jnp.exp(masked - log_total), 0.0)
    probs_b = lax.optimization_barrier(prob_full.astype(jnp.bfloat16)).astype(jnp.float32)
    attended = jnp.einsum('kgts,skd->tkgd', probs_b, value_heads)
    row_dots = lax.optimization_barrier(jnp.sum(grad_heads * attended, axis=-1))
    dprob = jnp.einsum('tkgd,skd->kgts', grad_heads, value_heads)
    dscore = prob_full * (dprob - jnp.transpose(row_dots, (1, 2, 0))[..., None])
    dscore_b = lax.optimization_barrier(dscore.astype(jnp.bfloat16)).astype(jnp.float32)
    grad_value = jnp.einsum('kgts,tkgd->skd', probs_b, grad_heads)
    grad_key = jnp.einsum('kgts,tkgd->skd', dscore_b, query_heads) * scaling
    grad_key = grad_key.reshape(seq_rows, KV_HEADS * HEAD_DIM).astype(jnp.bfloat16)
    grad_value = grad_value.reshape(seq_rows, KV_HEADS * HEAD_DIM).astype(jnp.bfloat16)
    contract = (((1,), (1,)), ((), ()))
    part_key = lax.dot_general(grad_key, wk, contract, preferred_element_type=jnp.float32)
    part_value = lax.dot_general(grad_value, wv, contract, preferred_element_type=jnp.float32)
    return part_key + part_value

def reference(inputs, query, grad_out, w_key, w_value, keep_mask):

    def section(packed):
        return one_section(packed[0], packed[1], packed[2], packed[3], packed[4], keep_mask)
    contribution = lax.map(section, (inputs, query, grad_out, w_key, w_value))
    return jnp.cumsum(contribution[::-1], axis=0)[::-1]
```

```python
import math

import jax
import jax.numpy as jnp
from jax import lax
from jax.sharding import PartitionSpec as P


def suffix_chain(own, axis):
    length, index = (lax.axis_size(axis), lax.axis_index(axis))
    total = own
    for k in range(length - 1):
        src_dev = length - 1 - k
        got = lax.ppermute(total.astype(jnp.bfloat16), axis, [(src_dev, src_dev - 1)])
        total = jnp.where(index == src_dev - 1, own + got.astype(jnp.float32), total)
    return total


def per_device(inputs, query, grad_out, w_key, w_value, keep_mask):
    tok_rows = inputs.shape[1]
    local_heads = query.shape[2]
    head_dim = query.shape[3]
    kv_cols = w_key.shape[2]
    kv_local = kv_cols // head_dim
    group_size = local_heads // kv_local
    scaling = 1.0 / math.sqrt(head_dim)
    tokens = inputs[0]
    key_rows = jnp.dot(tokens, w_key[0], preferred_element_type=jnp.float32).astype(jnp.bfloat16)
    value_rows = jnp.dot(tokens, w_value[0], preferred_element_type=jnp.float32).astype(
        jnp.bfloat16
    )
    kv_all = lax.all_gather(jnp.concatenate((key_rows, value_rows), axis=1), "ctx", axis=0, tiled=True)
    keys_all, values_all = kv_all[:, : key_rows.shape[1]], kv_all[:, key_rows.shape[1] :]
    seq_rows = keys_all.shape[0]
    key_heads = keys_all.reshape(seq_rows, kv_local, head_dim)
    value_heads = values_all.reshape(seq_rows, kv_local, head_dim)
    query_heads = query[0].reshape(tok_rows, kv_local, group_size, head_dim)
    grad_heads = grad_out[0].reshape(tok_rows, kv_local, group_size, head_dim)
    query_major = jnp.moveaxis(query_heads, 1, 0)
    grad_major = jnp.moveaxis(grad_heads, 1, 0)
    ctx_index = lax.axis_index("ctx")
    first_row = ctx_index * tok_rows
    row_pos = first_row + jnp.arange(tok_rows, dtype=jnp.int32)[:, None]
    col_pos = jnp.arange(seq_rows, dtype=jnp.int32)[None, :]
    allowed = (col_pos <= row_pos) & ((keep_mask[None, :] == 1) | (col_pos == row_pos))

    def one_group(packed):
        query_group, grad_group, key_group, value_group = packed
        scores = (
            jnp.einsum("tgd,sd->gts", query_group, key_group, preferred_element_type=jnp.float32)
            * scaling
        )
        masked = jnp.where(allowed, scores, -1e30)
        top_score = jnp.max(masked, axis=-1, keepdims=True)
        totals = jnp.sum(
            jnp.where(allowed, jnp.exp(masked - top_score), 0.0), axis=-1, keepdims=True
        )
        log_total = top_score + jnp.log(totals)
        prob_full = jnp.where(allowed, jnp.exp(masked - log_total), 0.0)
        prob_low = prob_full.astype(jnp.bfloat16)
        attended = jnp.einsum(
            "gts,sd->tgd", prob_low, value_group, preferred_element_type=jnp.float32
        )
        row_dots = jnp.sum(grad_group.astype(jnp.float32) * attended, axis=-1)
        dprob = jnp.einsum(
            "tgd,sd->gts", grad_group, value_group, preferred_element_type=jnp.float32
        )
        score_low = (prob_full * (dprob - jnp.transpose(row_dots, (1, 0))[..., None])).astype(
            jnp.bfloat16
        )
        return (prob_low, score_low)

    probs_b, dscore_b = lax.map(
        one_group,
        (query_major, grad_major, jnp.moveaxis(key_heads, 1, 0), jnp.moveaxis(value_heads, 1, 0)),
    )

    def per_group(packed):
        prob_group, score_group, query_group, grad_group = packed
        value_term = jnp.einsum(
            "gts,tgd->sd", prob_group, grad_group, preferred_element_type=jnp.float32
        )
        key_term = (
            jnp.einsum("gts,tgd->sd", score_group, query_group, preferred_element_type=jnp.float32)
            * scaling
        )
        return (key_term, value_term)

    key_term, value_term = lax.map(per_group, (probs_b, dscore_b, query_major, grad_major))
    key_flat = jnp.moveaxis(key_term, 0, 1).reshape(tok_rows * lax.axis_size("ctx"), kv_cols)
    value_flat = jnp.moveaxis(value_term, 0, 1).reshape(tok_rows * lax.axis_size("ctx"), kv_cols)
    key_grads = lax.psum_scatter(
        jnp.concatenate((key_flat, value_flat), axis=1).astype(jnp.bfloat16),
        "ctx",
        scatter_dimension=0,
        tiled=True,
    ).astype(jnp.float32)
    grad_key = key_grads[:, :kv_cols].astype(jnp.bfloat16)
    grad_value = key_grads[:, kv_cols:].astype(jnp.bfloat16)
    contract = (((1,), (1,)), ((), ()))
    partial_sum = lax.dot_general(grad_key, w_key[0], contract, preferred_element_type=jnp.float32)
    partial_sum = partial_sum + lax.dot_general(
        grad_value, w_value[0], contract, preferred_element_type=jnp.float32
    )
    reduced = lax.psum_scatter(
        partial_sum.astype(jnp.bfloat16), "head", scatter_dimension=1, tiled=True
    ).astype(jnp.float32)
    result = suffix_chain(reduced, "segment")
    return result[None]


def solution(mesh):
    return jax.shard_map(
        per_device,
        mesh=mesh,
        in_specs=(
            P("segment", "ctx", None),
            P("segment", "ctx", "head", None),
            P("segment", "ctx", "head", None),
            P("segment", None, "head"),
            P("segment", None, "head"),
            P(),
        ),
        out_specs=P("segment", "ctx", "head"),
        check_vma=False,
    )
```

```python
import math

import jax
import jax.numpy as jnp
from jax import lax
from jax.sharding import PartitionSpec as P


CHAIN_CHUNKS = 4


def shifted(x, axis, d, length, up):
    if up:
        perm = [(c, c + d) for c in range(length - d)]
    else:
        perm = [(c, c - d) for c in range(d, length)]
    return lax.ppermute(x, axis, perm)


def suffix_pipeline(own, axis, n_chunks):
    length, index = (lax.axis_size(axis), lax.axis_index(axis))
    rows, cols = own.shape
    width = cols // n_chunks
    out = jnp.zeros_like(own)
    recv = jnp.zeros((rows, width), jnp.bfloat16)
    perm = [(i, i - 1) for i in range(1, length)]
    steps = n_chunks + length - 1
    for tau in range(steps):
        k = tau - (length - 1 - index)
        valid = (k >= 0) & (k < n_chunks)
        start = jnp.clip(k, 0, n_chunks - 1) * width
        mine = lax.dynamic_slice_in_dim(own, start, width, axis=1)
        acc = mine + recv.astype(jnp.float32)
        cur = lax.dynamic_slice_in_dim(out, start, width, axis=1)
        out = lax.dynamic_update_slice_in_dim(out, jnp.where(valid, acc, cur), start, axis=1)
        if tau < steps - 1:
            recv = lax.ppermute(acc.astype(jnp.bfloat16), axis, perm)
    return out


def per_device(inputs, query, grad_out, w_key, w_value, keep_mask):
    tok_rows = inputs.shape[1]
    local_heads = query.shape[2]
    head_dim = query.shape[3]
    kv_cols = w_key.shape[2]
    kv_local = kv_cols // head_dim
    group_size = local_heads // kv_local
    scaling = 1.0 / math.sqrt(head_dim)
    ctx_len = lax.axis_size("ctx")
    ctx_index = lax.axis_index("ctx")
    tokens = inputs[0]
    key_rows = jnp.dot(tokens, w_key[0], preferred_element_type=jnp.float32).astype(jnp.bfloat16)
    value_rows = jnp.dot(tokens, w_value[0], preferred_element_type=jnp.float32).astype(
        jnp.bfloat16
    )
    kv_own = jnp.concatenate((key_rows, value_rows), axis=1)
    blocks = [kv_own] + [shifted(kv_own, "ctx", d, ctx_len, True) for d in range(1, ctx_len)]
    kv_all = jnp.concatenate(blocks, axis=0)
    seq_rows = kv_all.shape[0]
    key_heads = kv_all[:, :kv_cols].reshape(seq_rows, kv_local, head_dim)
    value_heads = kv_all[:, kv_cols:].reshape(seq_rows, kv_local, head_dim)
    query_heads = query[0].reshape(tok_rows, kv_local, group_size, head_dim)
    grad_heads = grad_out[0].reshape(tok_rows, kv_local, group_size, head_dim)
    query_major = jnp.moveaxis(query_heads, 1, 0)
    grad_major = jnp.moveaxis(grad_heads, 1, 0)
    first_row = ctx_index * tok_rows
    row_pos = first_row + jnp.arange(tok_rows, dtype=jnp.int32)[:, None]
    blk = jnp.arange(ctx_len, dtype=jnp.int32)
    col_pos = (
        (ctx_index - blk)[:, None] * tok_rows + jnp.arange(tok_rows, dtype=jnp.int32)[None, :]
    ).reshape(1, seq_rows)
    present = col_pos >= 0
    kept = jnp.take(keep_mask, jnp.clip(col_pos, 0, keep_mask.shape[0] - 1))
    allowed = present & (col_pos <= row_pos) & ((kept == 1) | (col_pos == row_pos))

    def one_group(packed):
        query_group, grad_group, key_group, value_group = packed
        scores = (
            jnp.einsum("tgd,sd->gts", query_group, key_group, preferred_element_type=jnp.float32)
            * scaling
        )
        masked = jnp.where(allowed, scores, -1e30)
        top_score = jnp.max(masked, axis=-1, keepdims=True)
        totals = jnp.sum(
            jnp.where(allowed, jnp.exp(masked - top_score), 0.0), axis=-1, keepdims=True
        )
        log_total = top_score + jnp.log(totals)
        prob_full = jnp.where(allowed, jnp.exp(masked - log_total), 0.0)
        prob_low = prob_full.astype(jnp.bfloat16)
        attended = jnp.einsum(
            "gts,sd->tgd", prob_low, value_group, preferred_element_type=jnp.float32
        )
        row_dots = jnp.sum(grad_group.astype(jnp.float32) * attended, axis=-1)
        dprob = jnp.einsum(
            "tgd,sd->gts", grad_group, value_group, preferred_element_type=jnp.float32
        )
        score_low = (prob_full * (dprob - jnp.transpose(row_dots, (1, 0))[..., None])).astype(
            jnp.bfloat16
        )
        return (prob_low, score_low)

    probs_b, dscore_b = lax.map(
        one_group,
        (query_major, grad_major, jnp.moveaxis(key_heads, 1, 0), jnp.moveaxis(value_heads, 1, 0)),
    )

    def per_group(packed):
        prob_group, score_group, query_group, grad_group = packed
        value_term = jnp.einsum(
            "gts,tgd->sd", prob_group, grad_group, preferred_element_type=jnp.float32
        )
        key_term = (
            jnp.einsum("gts,tgd->sd", score_group, query_group, preferred_element_type=jnp.float32)
            * scaling
        )
        return (key_term, value_term)

    key_term, value_term = lax.map(per_group, (probs_b, dscore_b, query_major, grad_major))
    key_flat = jnp.moveaxis(key_term, 0, 1).reshape(seq_rows, kv_cols)
    value_flat = jnp.moveaxis(value_term, 0, 1).reshape(seq_rows, kv_cols)
    terms = jnp.concatenate((key_flat, value_flat), axis=1)
    terms_low = terms.astype(jnp.bfloat16)
    kv_grad = terms[:tok_rows]
    for d in range(1, ctx_len):
        part = terms_low[d * tok_rows : (d + 1) * tok_rows]
        kv_grad = kv_grad + shifted(part, "ctx", d, ctx_len, False).astype(jnp.float32)
    grad_key = kv_grad[:, :kv_cols].astype(jnp.bfloat16)
    grad_value = kv_grad[:, kv_cols:].astype(jnp.bfloat16)
    contract = (((1,), (1,)), ((), ()))
    head_len = lax.axis_size("head")
    head_index = lax.axis_index("head")
    out_cols = w_key.shape[1] // head_len

    def partial_for(b):
        start = b * out_cols
        wk = lax.dynamic_slice_in_dim(w_key[0], start, out_cols, axis=0)
        wv = lax.dynamic_slice_in_dim(w_value[0], start, out_cols, axis=0)
        part = lax.dot_general(grad_key, wk, contract, preferred_element_type=jnp.float32)
        return part + lax.dot_general(grad_value, wv, contract, preferred_element_type=jnp.float32)

    received = []
    for d in range(1, head_len):
        target = lax.rem(head_index + d, head_len)
        send = partial_for(target).astype(jnp.bfloat16)
        perm = [(h, (h + d) % head_len) for h in range(head_len)]
        received.append(lax.ppermute(send, "head", perm))
    reduced = partial_for(head_index)
    for got in received:
        reduced = reduced + got.astype(jnp.float32)
    result = suffix_pipeline(reduced, "segment", CHAIN_CHUNKS)
    return result[None]


def solution(mesh):
    return jax.shard_map(
        per_device,
        mesh=mesh,
        in_specs=(
            P("segment", "ctx", None),
            P("segment", "ctx", "head", None),
            P("segment", "ctx", "head", None),
            P("segment", None, "head"),
            P("segment", None, "head"),
            P(),
        ),
        out_specs=P("segment", "ctx", "head"),
        check_vma=False,
    )
```

```python
import math

import jax
import jax.numpy as jnp
from jax import lax
from jax.sharding import PartitionSpec as P


CHAIN_CHUNKS = 4


def shifted(x, axis, d, length, up):
    if up:
        perm = [(c, c + d) for c in range(length - d)]
    else:
        perm = [(c, c - d) for c in range(d, length)]
    return lax.ppermute(x, axis, perm)


def suffix_pipeline(own, axis, n_chunks):
    length, index = (lax.axis_size(axis), lax.axis_index(axis))
    rows, cols = own.shape
    height = rows // n_chunks
    chunks = own.reshape(n_chunks, height, cols)
    pad = jnp.zeros((length - 1, height, cols), own.dtype)
    padded = jnp.concatenate((pad, chunks, pad), axis=0)
    steps = n_chunks + length - 1
    ordered = lax.dynamic_slice_in_dim(padded, index, steps, axis=0)
    perm = [(i, i - 1) for i in range(1, length)]
    recv = jnp.zeros((height, cols), jnp.bfloat16)
    done = []
    for tau in range(steps):
        acc = ordered[tau] + recv.astype(jnp.float32)
        done.append(acc)
        if tau < steps - 1:
            recv = lax.ppermute(acc.astype(jnp.bfloat16), axis, perm)
    stacked = jnp.stack(done, axis=0)
    mine = lax.dynamic_slice_in_dim(stacked, length - 1 - index, n_chunks, axis=0)
    return mine.reshape(rows, cols)


def per_device(inputs, query, grad_out, w_key, w_value, keep_mask):
    tok_rows = inputs.shape[1]
    local_heads = query.shape[2]
    head_dim = query.shape[3]
    kv_cols = w_key.shape[2]
    kv_local = kv_cols // head_dim
    group_size = local_heads // kv_local
    scaling = 1.0 / math.sqrt(head_dim)
    ctx_len = lax.axis_size("ctx")
    ctx_index = lax.axis_index("ctx")
    tokens = inputs[0]
    key_rows = jnp.dot(tokens, w_key[0], preferred_element_type=jnp.float32).astype(jnp.bfloat16)
    value_rows = jnp.dot(tokens, w_value[0], preferred_element_type=jnp.float32).astype(
        jnp.bfloat16
    )
    kv_own = jnp.concatenate((key_rows, value_rows), axis=1)
    blocks = [kv_own] + [shifted(kv_own, "ctx", d, ctx_len, True) for d in range(1, ctx_len)]
    kv_all = jnp.concatenate(blocks, axis=0)
    seq_rows = kv_all.shape[0]
    key_heads = kv_all[:, :kv_cols].reshape(seq_rows, kv_local, head_dim)
    value_heads = kv_all[:, kv_cols:].reshape(seq_rows, kv_local, head_dim)
    query_heads = query[0].reshape(tok_rows, kv_local, group_size, head_dim)
    grad_heads = grad_out[0].reshape(tok_rows, kv_local, group_size, head_dim)
    query_major = jnp.moveaxis(query_heads, 1, 0)
    grad_major = jnp.moveaxis(grad_heads, 1, 0)
    first_row = ctx_index * tok_rows
    row_pos = first_row + jnp.arange(tok_rows, dtype=jnp.int32)[:, None]
    blk = jnp.arange(ctx_len, dtype=jnp.int32)
    col_pos = (
        (ctx_index - blk)[:, None] * tok_rows + jnp.arange(tok_rows, dtype=jnp.int32)[None, :]
    ).reshape(1, seq_rows)
    present = col_pos >= 0
    keep_blocks = keep_mask.reshape(ctx_len, tok_rows)
    kept = jnp.concatenate(
        [
            lax.dynamic_index_in_dim(keep_blocks, jnp.maximum(ctx_index - p, 0), 0, keepdims=True)
            for p in range(ctx_len)
        ],
        axis=1,
    )
    allowed = present & (col_pos <= row_pos) & ((kept == 1) | (col_pos == row_pos))
    allowed = lax.optimization_barrier(allowed)

    def one_group(packed):
        query_group, grad_group, key_group, value_group = packed
        scores = (
            jnp.einsum("tgd,sd->gts", query_group, key_group, preferred_element_type=jnp.float32)
            * scaling
        )
        masked = jnp.where(allowed, scores, -1e30)
        top_score = jnp.max(masked, axis=-1, keepdims=True)
        totals = jnp.sum(
            jnp.where(allowed, jnp.exp(masked - top_score), 0.0), axis=-1, keepdims=True
        )
        log_total = top_score + jnp.log(totals)
        prob_full = jnp.where(allowed, jnp.exp(masked - log_total), 0.0)
        prob_low = prob_full.astype(jnp.bfloat16)
        attended = jnp.einsum(
            "gts,sd->tgd", prob_low, value_group, preferred_element_type=jnp.float32
        )
        row_dots = jnp.sum(grad_group.astype(jnp.float32) * attended, axis=-1)
        dprob = jnp.einsum(
            "tgd,sd->gts", grad_group, value_group, preferred_element_type=jnp.float32
        )
        score_low = (prob_full * (dprob - jnp.transpose(row_dots, (1, 0))[..., None])).astype(
            jnp.bfloat16
        )
        return (prob_low, score_low)

    probs_b, dscore_b = lax.map(
        one_group,
        (query_major, grad_major, jnp.moveaxis(key_heads, 1, 0), jnp.moveaxis(value_heads, 1, 0)),
    )

    def per_group(packed):
        prob_group, score_group, query_group, grad_group = packed
        value_term = jnp.einsum(
            "gts,tgd->sd", prob_group, grad_group, preferred_element_type=jnp.float32
        )
        key_term = (
            jnp.einsum("gts,tgd->sd", score_group, query_group, preferred_element_type=jnp.float32)
            * scaling
        )
        return (key_term, value_term)

    key_term, value_term = lax.map(per_group, (probs_b, dscore_b, query_major, grad_major))
    key_flat = jnp.moveaxis(key_term, 0, 1).reshape(seq_rows, kv_cols)
    value_flat = jnp.moveaxis(value_term, 0, 1).reshape(seq_rows, kv_cols)
    terms = jnp.concatenate((key_flat, value_flat), axis=1)
    terms_low = terms.astype(jnp.bfloat16)
    kv_grad = terms[:tok_rows]
    for d in range(1, ctx_len):
        part = terms_low[d * tok_rows : (d + 1) * tok_rows]
        kv_grad = kv_grad + shifted(part, "ctx", d, ctx_len, False).astype(jnp.float32)
    grad_key = kv_grad[:, :kv_cols].astype(jnp.bfloat16)
    grad_value = kv_grad[:, kv_cols:].astype(jnp.bfloat16)
    contract = (((1,), (1,)), ((), ()))
    head_len = lax.axis_size("head")
    head_index = lax.axis_index("head")
    out_cols = w_key.shape[1] // head_len

    def partial_for(b):
        start = b * out_cols
        wk = lax.dynamic_slice_in_dim(w_key[0], start, out_cols, axis=0)
        wv = lax.dynamic_slice_in_dim(w_value[0], start, out_cols, axis=0)
        part = lax.dot_general(grad_key, wk, contract, preferred_element_type=jnp.float32)
        return part + lax.dot_general(grad_value, wv, contract, preferred_element_type=jnp.float32)

    received = []
    for d in range(1, head_len):
        target = lax.rem(head_index + d, head_len)
        send = partial_for(target).astype(jnp.bfloat16)
        perm = [(h, (h + d) % head_len) for h in range(head_len)]
        received.append(lax.ppermute(send, "head", perm))
    reduced = partial_for(head_index)
    for got in received:
        reduced = reduced + got.astype(jnp.float32)
    result = suffix_pipeline(reduced, "segment", CHAIN_CHUNKS)
    return result[None]


def solution(mesh):
    return jax.shard_map(
        per_device,
        mesh=mesh,
        in_specs=(
            P("segment", "ctx", None),
            P("segment", "ctx", "head", None),
            P("segment", "ctx", "head", None),
            P("segment", None, "head"),
            P("segment", None, "head"),
            P(),
        ),
        out_specs=P("segment", "ctx", "head"),
        check_vma=False,
    )
```

```python
import math

import jax
import jax.numpy as jnp
from jax import lax
from jax.sharding import PartitionSpec as P


CHAIN_CHUNKS = 2


def shifted(x, axis, d, length, up):
    if up:
        perm = [(c, c + d) for c in range(length - d)]
    else:
        perm = [(c, c - d) for c in range(d, length)]
    return lax.ppermute(x, axis, perm)


def suffix_pipeline(own, axis, n_chunks):
    length, index = (lax.axis_size(axis), lax.axis_index(axis))
    rows, cols = own.shape
    height = rows // n_chunks
    chunks = own.reshape(n_chunks, height, cols)
    pad = jnp.zeros((length - 1, height, cols), own.dtype)
    padded = jnp.concatenate((pad, chunks, pad), axis=0)
    steps = n_chunks + length - 1
    ordered = lax.dynamic_slice_in_dim(padded, index, steps, axis=0)
    perm = [(i, i - 1) for i in range(1, length)]
    recv = jnp.zeros((height, cols), jnp.bfloat16)
    done = []
    for tau in range(steps):
        acc = ordered[tau] + recv.astype(jnp.float32)
        done.append(acc)
        if tau < steps - 1:
            recv = lax.ppermute(acc.astype(jnp.bfloat16), axis, perm)
    stacked = jnp.stack(done, axis=0)
    mine = lax.dynamic_slice_in_dim(stacked, length - 1 - index, n_chunks, axis=0)
    return mine.reshape(rows, cols)


def per_device(inputs, query, grad_out, w_key, w_value, keep_mask):
    tok_rows = inputs.shape[1]
    local_heads = query.shape[2]
    head_dim = query.shape[3]
    kv_cols = w_key.shape[2]
    kv_local = kv_cols // head_dim
    group_size = local_heads // kv_local
    scaling = 1.0 / math.sqrt(head_dim)
    ctx_len = lax.axis_size("ctx")
    ctx_index = lax.axis_index("ctx")
    tokens = inputs[0]
    key_rows = jnp.dot(tokens, w_key[0], preferred_element_type=jnp.float32).astype(jnp.bfloat16)
    value_rows = jnp.dot(tokens, w_value[0], preferred_element_type=jnp.float32).astype(
        jnp.bfloat16
    )
    kv_own = jnp.concatenate((key_rows, value_rows), axis=1)
    blocks = [kv_own] + [shifted(kv_own, "ctx", d, ctx_len, True) for d in range(1, ctx_len)]
    kv_all = jnp.concatenate(blocks, axis=0)
    seq_rows = kv_all.shape[0]
    key_heads = kv_all[:, :kv_cols].reshape(seq_rows, kv_local, head_dim)
    value_heads = kv_all[:, kv_cols:].reshape(seq_rows, kv_local, head_dim)
    query_heads = query[0].reshape(tok_rows, kv_local, group_size, head_dim)
    grad_heads = grad_out[0].reshape(tok_rows, kv_local, group_size, head_dim)
    query_major = jnp.moveaxis(query_heads, 1, 0)
    grad_major = jnp.moveaxis(grad_heads, 1, 0)
    first_row = ctx_index * tok_rows
    row_pos = first_row + jnp.arange(tok_rows, dtype=jnp.int32)[:, None]
    blk = jnp.arange(ctx_len, dtype=jnp.int32)
    col_pos = (
        (ctx_index - blk)[:, None] * tok_rows + jnp.arange(tok_rows, dtype=jnp.int32)[None, :]
    ).reshape(1, seq_rows)
    present = col_pos >= 0
    keep_blocks = keep_mask.reshape(ctx_len, tok_rows)
    kept = jnp.concatenate(
        [
            lax.dynamic_index_in_dim(keep_blocks, jnp.maximum(ctx_index - p, 0), 0, keepdims=True)
            for p in range(ctx_len)
        ],
        axis=1,
    )
    allowed = present & (col_pos <= row_pos) & ((kept == 1) | (col_pos == row_pos))
    allowed = lax.optimization_barrier(allowed)

    key_major = jnp.moveaxis(key_heads, 1, 0)
    value_major = jnp.moveaxis(value_heads, 1, 0)
    scores = (
        jnp.einsum("ktgd,ksd->kgts", query_major, key_major, preferred_element_type=jnp.float32)
        * scaling
    )
    masked = jnp.where(allowed, scores, -1e30)
    top_score = jnp.max(masked, axis=-1, keepdims=True)
    totals = jnp.sum(jnp.where(allowed, jnp.exp(masked - top_score), 0.0), axis=-1, keepdims=True)
    log_total = top_score + jnp.log(totals)
    prob_full = jnp.where(allowed, jnp.exp(masked - log_total), 0.0)
    probs_b = prob_full.astype(jnp.bfloat16)
    attended = jnp.einsum("kgts,ksd->ktgd", probs_b, value_major, preferred_element_type=jnp.float32)
    row_dots = jnp.sum(grad_major.astype(jnp.float32) * attended, axis=-1)
    dprob = jnp.einsum("ktgd,ksd->kgts", grad_major, value_major, preferred_element_type=jnp.float32)
    dscore_b = (prob_full * (dprob - jnp.transpose(row_dots, (0, 2, 1))[..., None])).astype(
        jnp.bfloat16
    )
    value_term = jnp.einsum("kgts,ktgd->ksd", probs_b, grad_major, preferred_element_type=jnp.float32)
    key_term = (
        jnp.einsum("kgts,ktgd->ksd", dscore_b, query_major, preferred_element_type=jnp.float32)
        * scaling
    )
    key_flat = jnp.moveaxis(key_term, 0, 1).reshape(seq_rows, kv_cols)
    value_flat = jnp.moveaxis(value_term, 0, 1).reshape(seq_rows, kv_cols)
    terms = jnp.concatenate((key_flat, value_flat), axis=1)
    terms_low = terms.astype(jnp.bfloat16)
    kv_grad = terms[:tok_rows]
    for d in range(1, ctx_len):
        part = terms_low[d * tok_rows : (d + 1) * tok_rows]
        kv_grad = kv_grad + shifted(part, "ctx", d, ctx_len, False).astype(jnp.float32)
    grad_key = kv_grad[:, :kv_cols].astype(jnp.bfloat16)
    grad_value = kv_grad[:, kv_cols:].astype(jnp.bfloat16)
    contract = (((1,), (1,)), ((), ()))
    head_len = lax.axis_size("head")
    head_index = lax.axis_index("head")
    out_cols = w_key.shape[1] // head_len

    def partial_for(b):
        start = b * out_cols
        wk = lax.dynamic_slice_in_dim(w_key[0], start, out_cols, axis=0)
        wv = lax.dynamic_slice_in_dim(w_value[0], start, out_cols, axis=0)
        part = lax.dot_general(grad_key, wk, contract, preferred_element_type=jnp.float32)
        return part + lax.dot_general(grad_value, wv, contract, preferred_element_type=jnp.float32)

    received = []
    for d in range(1, head_len):
        target = lax.rem(head_index + d, head_len)
        send = partial_for(target).astype(jnp.bfloat16)
        perm = [(h, (h + d) % head_len) for h in range(head_len)]
        received.append(lax.ppermute(send, "head", perm))
    reduced = partial_for(head_index)
    for got in received:
        reduced = reduced + got.astype(jnp.float32)
    result = suffix_pipeline(reduced, "segment", CHAIN_CHUNKS)
    return result[None]


def solution(mesh):
    return jax.shard_map(
        per_device,
        mesh=mesh,
        in_specs=(
            P("segment", "ctx", None),
            P("segment", "ctx", "head", None),
            P("segment", "ctx", "head", None),
            P("segment", None, "head"),
            P("segment", None, "head"),
            P(),
        ),
        out_specs=P("segment", "ctx", "head"),
        check_vma=False,
    )
```

```python
import math

import jax
import jax.numpy as jnp
from jax import lax
from jax.experimental import pallas as pl
from jax.sharding import PartitionSpec as P


CHAIN_CHUNKS = 2


def shifted(x, axis, d, length, up):
    if up:
        perm = [(c, c + d) for c in range(length - d)]
    else:
        perm = [(c, c - d) for c in range(d, length)]
    return lax.ppermute(x, axis, perm)


def suffix_pipeline(own, axis, n_chunks):
    length, index = (lax.axis_size(axis), lax.axis_index(axis))
    rows, cols = own.shape
    height = rows // n_chunks
    chunks = own.reshape(n_chunks, height, cols)
    pad = jnp.zeros((length - 1, height, cols), own.dtype)
    padded = jnp.concatenate((pad, chunks, pad), axis=0)
    steps = n_chunks + length - 1
    ordered = lax.dynamic_slice_in_dim(padded, index, steps, axis=0)
    perm = [(i, i - 1) for i in range(1, length)]
    recv = jnp.zeros((height, cols), jnp.bfloat16)
    done = []
    for tau in range(steps):
        acc = ordered[tau] + recv.astype(jnp.float32)
        done.append(acc)
        if tau < steps - 1:
            recv = lax.ppermute(acc.astype(jnp.bfloat16), axis, perm)
    stacked = jnp.stack(done, axis=0)
    mine = lax.dynamic_slice_in_dim(stacked, length - 1 - index, n_chunks, axis=0)
    return mine.reshape(rows, cols)


def attention_terms(q2, g2, kv_all, allowed_t, kv_local, group, head_dim, scaling):
    seq_rows = kv_all.shape[0]
    kv_cols = kv_local * head_dim
    nt = (((1,), (1,)), ((), ()))

    def kernel(q_ref, g_ref, kv_ref, m_ref, out_ref):
        allowed = m_ref[...] > 0.5
        for k in range(kv_local):
            key = kv_ref[:, k * head_dim : (k + 1) * head_dim]
            val = kv_ref[:, kv_cols + k * head_dim : kv_cols + (k + 1) * head_dim]
            dk = jnp.zeros((seq_rows, head_dim), jnp.float32)
            dv = jnp.zeros((seq_rows, head_dim), jnp.float32)
            for j in range(group):
                h = k * group + j
                q = q_ref[:, h * head_dim : (h + 1) * head_dim]
                gr = g_ref[:, h * head_dim : (h + 1) * head_dim]
                s = lax.dot_general(key, q, nt, preferred_element_type=jnp.float32) * scaling
                masked = jnp.where(allowed, s, -1e30)
                top = jnp.max(masked, axis=0, keepdims=True)
                tot = jnp.sum(jnp.where(allowed, jnp.exp(masked - top), 0.0), axis=0, keepdims=True)
                log_total = top + jnp.log(tot)
                p = jnp.where(allowed, jnp.exp(masked - log_total), 0.0)
                pb = p.astype(jnp.bfloat16)
                dp = lax.dot_general(val, gr, nt, preferred_element_type=jnp.float32)
                rd = jnp.sum(pb.astype(jnp.float32) * dp, axis=0, keepdims=True)
                ds = (p * (dp - rd)).astype(jnp.bfloat16)
                dv = dv + jnp.dot(pb, gr, preferred_element_type=jnp.float32)
                dk = dk + jnp.dot(ds, q, preferred_element_type=jnp.float32)
            out_ref[:, k * head_dim : (k + 1) * head_dim] = dk * scaling
            out_ref[:, kv_cols + k * head_dim : kv_cols + (k + 1) * head_dim] = dv

    return pl.pallas_call(
        kernel, out_shape=jax.ShapeDtypeStruct((seq_rows, 2 * kv_cols), jnp.float32)
    )(q2, g2, kv_all, allowed_t)


def per_device(inputs, query, grad_out, w_key, w_value, keep_mask):
    tok_rows = inputs.shape[1]
    local_heads = query.shape[2]
    head_dim = query.shape[3]
    kv_cols = w_key.shape[2]
    kv_local = kv_cols // head_dim
    group_size = local_heads // kv_local
    scaling = 1.0 / math.sqrt(head_dim)
    ctx_len = lax.axis_size("ctx")
    ctx_index = lax.axis_index("ctx")
    tokens = inputs[0]
    key_rows = jnp.dot(tokens, w_key[0], preferred_element_type=jnp.float32).astype(jnp.bfloat16)
    value_rows = jnp.dot(tokens, w_value[0], preferred_element_type=jnp.float32).astype(
        jnp.bfloat16
    )
    kv_own = jnp.concatenate((key_rows, value_rows), axis=1)
    blocks = [kv_own] + [shifted(kv_own, "ctx", d, ctx_len, True) for d in range(1, ctx_len)]
    kv_all = jnp.concatenate(blocks, axis=0)
    seq_rows = kv_all.shape[0]
    first_row = ctx_index * tok_rows
    row_pos = first_row + jnp.arange(tok_rows, dtype=jnp.int32)[None, :]
    blk = jnp.arange(ctx_len, dtype=jnp.int32)
    col_pos = (
        (ctx_index - blk)[:, None] * tok_rows + jnp.arange(tok_rows, dtype=jnp.int32)[None, :]
    ).reshape(seq_rows, 1)
    present = col_pos >= 0
    keep_blocks = keep_mask.reshape(ctx_len, tok_rows)
    kept = jnp.concatenate(
        [
            lax.dynamic_index_in_dim(keep_blocks, jnp.maximum(ctx_index - p, 0), 0, keepdims=False)
            for p in range(ctx_len)
        ],
        axis=0,
    ).reshape(seq_rows, 1)
    allowed_t = present & (col_pos <= row_pos) & ((kept == 1) | (col_pos == row_pos))
    q2 = query[0].reshape(tok_rows, local_heads * head_dim)
    g2 = grad_out[0].reshape(tok_rows, local_heads * head_dim)
    terms = attention_terms(
        q2, g2, kv_all, allowed_t.astype(jnp.float32), kv_local, group_size, head_dim, scaling
    )
    terms_low = terms.astype(jnp.bfloat16)
    kv_grad = terms[:tok_rows]
    for d in range(1, ctx_len):
        part = terms_low[d * tok_rows : (d + 1) * tok_rows]
        kv_grad = kv_grad + shifted(part, "ctx", d, ctx_len, False).astype(jnp.float32)
    grad_key = kv_grad[:, :kv_cols].astype(jnp.bfloat16)
    grad_value = kv_grad[:, kv_cols:].astype(jnp.bfloat16)
    contract = (((1,), (1,)), ((), ()))
    head_len = lax.axis_size("head")
    head_index = lax.axis_index("head")
    out_cols = w_key.shape[1] // head_len

    def partial_for(b):
        start = b * out_cols
        wk = lax.dynamic_slice_in_dim(w_key[0], start, out_cols, axis=0)
        wv = lax.dynamic_slice_in_dim(w_value[0], start, out_cols, axis=0)
        part = lax.dot_general(grad_key, wk, contract, preferred_element_type=jnp.float32)
        return part + lax.dot_general(grad_value, wv, contract, preferred_element_type=jnp.float32)

    received = []
    for d in range(1, head_len):
        target = lax.rem(head_index + d, head_len)
        send = partial_for(target).astype(jnp.bfloat16)
        perm = [(h, (h + d) % head_len) for h in range(head_len)]
        received.append(lax.ppermute(send, "head", perm))
    reduced = partial_for(head_index)
    for got in received:
        reduced = reduced + got.astype(jnp.float32)
    result = suffix_pipeline(reduced, "segment", CHAIN_CHUNKS)
    return result[None]


def solution(mesh):
    return jax.shard_map(
        per_device,
        mesh=mesh,
        in_specs=(
            P("segment", "ctx", None),
            P("segment", "ctx", "head", None),
            P("segment", "ctx", "head", None),
            P("segment", None, "head"),
            P("segment", None, "head"),
            P(),
        ),
        out_specs=P("segment", "ctx", "head"),
        check_vma=False,
    )
```

```python
import math

import jax
import jax.numpy as jnp
from jax import lax
from jax.experimental import pallas as pl
from jax.sharding import PartitionSpec as P


CHAIN_CHUNKS = 2


def shifted(x, axis, d, length, up):
    if up:
        perm = [(c, c + d) for c in range(length - d)]
    else:
        perm = [(c, c - d) for c in range(d, length)]
    return lax.ppermute(x, axis, perm)


def suffix_pipeline(own, axis, n_chunks):
    length, index = (lax.axis_size(axis), lax.axis_index(axis))
    rows, cols = own.shape
    height = rows // n_chunks
    chunks = own.reshape(n_chunks, height, cols)
    pad = jnp.zeros((length - 1, height, cols), own.dtype)
    padded = jnp.concatenate((pad, chunks, pad), axis=0)
    steps = n_chunks + length - 1
    ordered = lax.dynamic_slice_in_dim(padded, index, steps, axis=0)
    perm = [(i, i - 1) for i in range(1, length)]
    recv = jnp.zeros((height, cols), jnp.bfloat16)
    done = []
    for tau in range(steps):
        acc = ordered[tau] + recv.astype(jnp.float32)
        done.append(acc)
        if tau < steps - 1:
            recv = lax.ppermute(acc.astype(jnp.bfloat16), axis, perm)
    stacked = jnp.stack(done, axis=0)
    mine = lax.dynamic_slice_in_dim(stacked, length - 1 - index, n_chunks, axis=0)
    return mine.reshape(rows, cols)


def attention_terms(q3, g3, kv_blocks, lower, upper, kv_local, head_dim, scaling):
    tok_rows = q3.shape[1]
    group = q3.shape[0] // kv_local
    n_blocks = len(kv_blocks)
    seq_rows = tok_rows * n_blocks
    kv_cols = kv_local * head_dim
    nt = (((1,), (1,)), ((), ()))

    def kernel(*refs):
        q_ref, g_ref = refs[0], refs[1]
        kv_refs = refs[2 : 2 + n_blocks]
        lo_ref, hi_ref, low_ref, own_ref = refs[2 + n_blocks :]
        rows = lax.broadcasted_iota(jnp.int32, (seq_rows, tok_rows), 1)
        allowed = (lo_ref[...] <= rows) & (rows <= hi_ref[...])
        for k in range(kv_local):
            kcols = slice(k * head_dim, (k + 1) * head_dim)
            vcols = slice(kv_cols + k * head_dim, kv_cols + (k + 1) * head_dim)
            key = jnp.concatenate([r[:, kcols] for r in kv_refs], axis=0)
            val = jnp.concatenate([r[:, vcols] for r in kv_refs], axis=0)
            dk = jnp.zeros((seq_rows, head_dim), jnp.float32)
            dv = jnp.zeros((seq_rows, head_dim), jnp.float32)
            for j in range(group):
                h = k * group + j
                q = q_ref[h]
                gr = g_ref[h]
                s = lax.dot_general(key, q, nt, preferred_element_type=jnp.float32) * scaling
                masked = jnp.where(allowed, s, -1e30)
                top = jnp.max(masked, axis=0, keepdims=True)
                tot = jnp.sum(jnp.where(allowed, jnp.exp(masked - top), 0.0), axis=0, keepdims=True)
                log_total = top + jnp.log(tot)
                p = jnp.where(allowed, jnp.exp(masked - log_total), 0.0)
                pb = p.astype(jnp.bfloat16)
                dp = lax.dot_general(val, gr, nt, preferred_element_type=jnp.float32)
                rd = jnp.sum(pb.astype(jnp.float32) * dp, axis=0, keepdims=True)
                ds = (p * (dp - rd)).astype(jnp.bfloat16)
                dv = dv + jnp.dot(pb, gr, preferred_element_type=jnp.float32)
                dk = dk + jnp.dot(ds, q, preferred_element_type=jnp.float32)
            dk = dk * scaling
            low_ref[:, kcols] = dk.astype(jnp.bfloat16)
            low_ref[:, vcols] = dv.astype(jnp.bfloat16)
            own_ref[:, kcols] = dk[:tok_rows]
            own_ref[:, vcols] = dv[:tok_rows]

    return pl.pallas_call(
        kernel,
        out_shape=(
            jax.ShapeDtypeStruct((seq_rows, 2 * kv_cols), jnp.bfloat16),
            jax.ShapeDtypeStruct((tok_rows, 2 * kv_cols), jnp.float32),
        ),
    )(q3, g3, *kv_blocks, lower, upper)


def per_device(inputs, query, grad_out, w_key, w_value, keep_mask):
    tok_rows = inputs.shape[1]
    local_heads = query.shape[2]
    head_dim = query.shape[3]
    kv_cols = w_key.shape[2]
    kv_local = kv_cols // head_dim
    group_size = local_heads // kv_local
    scaling = 1.0 / math.sqrt(head_dim)
    ctx_len = lax.axis_size("ctx")
    ctx_index = lax.axis_index("ctx")
    tokens = inputs[0]
    key_rows = jnp.dot(tokens, w_key[0], preferred_element_type=jnp.float32).astype(jnp.bfloat16)
    value_rows = jnp.dot(tokens, w_value[0], preferred_element_type=jnp.float32).astype(
        jnp.bfloat16
    )
    kv_own = jnp.concatenate((key_rows, value_rows), axis=1)
    blocks = [kv_own] + [shifted(kv_own, "ctx", d, ctx_len, True) for d in range(1, ctx_len)]
    seq_rows = tok_rows * ctx_len
    first_row = ctx_index * tok_rows
    blk = jnp.arange(ctx_len, dtype=jnp.int32)
    col_pos = (
        (ctx_index - blk)[:, None] * tok_rows + jnp.arange(tok_rows, dtype=jnp.int32)[None, :]
    ).reshape(seq_rows, 1)
    keep_blocks = keep_mask.reshape(ctx_len, tok_rows)
    kept = jnp.concatenate(
        [
            lax.dynamic_index_in_dim(keep_blocks, jnp.maximum(ctx_index - p, 0), 0, keepdims=False)
            for p in range(ctx_len)
        ],
        axis=0,
    ).reshape(seq_rows, 1)
    never = jnp.iinfo(jnp.int32).max
    lower = jnp.where(col_pos >= 0, col_pos - first_row, never)
    upper = jnp.where(kept == 1, never, col_pos - first_row)
    q3 = jnp.transpose(query[0], (1, 0, 2))
    g3 = jnp.transpose(grad_out[0], (1, 0, 2))
    terms_low, kv_grad = attention_terms(
        q3, g3, blocks, lower, upper, kv_local, head_dim, scaling
    )
    for d in range(1, ctx_len):
        part = terms_low[d * tok_rows : (d + 1) * tok_rows]
        kv_grad = kv_grad + shifted(part, "ctx", d, ctx_len, False).astype(jnp.float32)
    grad_key = kv_grad[:, :kv_cols].astype(jnp.bfloat16)
    grad_value = kv_grad[:, kv_cols:].astype(jnp.bfloat16)
    contract = (((1,), (1,)), ((), ()))
    head_len = lax.axis_size("head")
    head_index = lax.axis_index("head")
    out_cols = w_key.shape[1] // head_len

    def partial_for(b):
        start = b * out_cols
        wk = lax.dynamic_slice_in_dim(w_key[0], start, out_cols, axis=0)
        wv = lax.dynamic_slice_in_dim(w_value[0], start, out_cols, axis=0)
        part = lax.dot_general(grad_key, wk, contract, preferred_element_type=jnp.float32)
        return part + lax.dot_general(grad_value, wv, contract, preferred_element_type=jnp.float32)

    received = []
    for d in range(1, head_len):
        target = lax.rem(head_index + d, head_len)
        send = partial_for(target).astype(jnp.bfloat16)
        perm = [(h, (h + d) % head_len) for h in range(head_len)]
        received.append(lax.ppermute(send, "head", perm))
    reduced = partial_for(head_index)
    for got in received:
        reduced = reduced + got.astype(jnp.float32)
    result = suffix_pipeline(reduced, "segment", CHAIN_CHUNKS)
    return result[None]


def solution(mesh):
    return jax.shard_map(
        per_device,
        mesh=mesh,
        in_specs=(
            P("segment", "ctx", None),
            P("segment", "ctx", "head", None),
            P("segment", "ctx", "head", None),
            P("segment", None, "head"),
            P("segment", None, "head"),
            P(),
        ),
        out_specs=P("segment", "ctx", "head"),
        check_vma=False,
    )
```

```python
import math

import jax
import jax.numpy as jnp
from jax import lax
from jax.experimental import pallas as pl
from jax.sharding import PartitionSpec as P


CHAIN_CHUNKS = 2


def shifted(x, axis, d, length, up):
    if up:
        perm = [(c, c + d) for c in range(length - d)]
    else:
        perm = [(c, c - d) for c in range(d, length)]
    return lax.ppermute(x, axis, perm)


def suffix_pipeline(own, axis, n_chunks):
    length, index = (lax.axis_size(axis), lax.axis_index(axis))
    rows, cols = own.shape
    height = rows // n_chunks
    chunks = own.reshape(n_chunks, height, cols)
    pad = jnp.zeros((length - 1, height, cols), own.dtype)
    padded = jnp.concatenate((pad, chunks, pad), axis=0)
    steps = n_chunks + length - 1
    ordered = lax.dynamic_slice_in_dim(padded, index, steps, axis=0)
    recv = jnp.zeros((height, cols), jnp.bfloat16)
    done = []
    for tau in range(steps):
        acc = ordered[tau] + recv.astype(jnp.float32)
        done.append(acc)
        perm = [(i, i - 1) for i in range(1, length) if 0 <= tau - (length - 1 - i) < n_chunks]
        if perm:
            recv = lax.ppermute(acc.astype(jnp.bfloat16), axis, perm)
    stacked = jnp.stack(done, axis=0)
    mine = lax.dynamic_slice_in_dim(stacked, length - 1 - index, n_chunks, axis=0)
    return mine.reshape(rows, cols)


def attention_terms(q3, g3, kv_blocks, lower, upper, kv_local, head_dim, scaling):
    tok_rows = q3.shape[1]
    group = q3.shape[0] // kv_local
    n_blocks = len(kv_blocks)
    seq_rows = tok_rows * n_blocks
    kv_cols = kv_local * head_dim
    nt = (((1,), (1,)), ((), ()))

    def kernel(*refs):
        q_ref, g_ref = refs[0], refs[1]
        kv_refs = refs[2 : 2 + n_blocks]
        lo_ref, hi_ref, low_ref, own_ref = refs[2 + n_blocks :]
        rows = lax.broadcasted_iota(jnp.int32, (seq_rows, tok_rows), 1)
        allowed = (lo_ref[...] <= rows) & (rows <= hi_ref[...])
        for k in range(kv_local):
            kcols = slice(k * head_dim, (k + 1) * head_dim)
            vcols = slice(kv_cols + k * head_dim, kv_cols + (k + 1) * head_dim)
            key = jnp.concatenate([r[:, kcols] for r in kv_refs], axis=0)
            val = jnp.concatenate([r[:, vcols] for r in kv_refs], axis=0)
            dk = jnp.zeros((seq_rows, head_dim), jnp.float32)
            dv = jnp.zeros((seq_rows, head_dim), jnp.float32)
            for j in range(group):
                h = k * group + j
                q = q_ref[h]
                gr = g_ref[h]
                s = lax.dot_general(key, q, nt, preferred_element_type=jnp.float32) * scaling
                masked = jnp.where(allowed, s, -1e30)
                top = jnp.max(masked, axis=0, keepdims=True)
                tot = jnp.sum(jnp.where(allowed, jnp.exp(masked - top), 0.0), axis=0, keepdims=True)
                log_total = top + jnp.log(tot)
                p = jnp.where(allowed, jnp.exp(masked - log_total), 0.0)
                pb = p.astype(jnp.bfloat16)
                dp = lax.dot_general(val, gr, nt, preferred_element_type=jnp.float32)
                rd = jnp.sum(pb.astype(jnp.float32) * dp, axis=0, keepdims=True)
                ds = (p * (dp - rd)).astype(jnp.bfloat16)
                dv = dv + jnp.dot(pb, gr, preferred_element_type=jnp.float32)
                dk = dk + jnp.dot(ds, q, preferred_element_type=jnp.float32)
            dk = dk * scaling
            low_ref[:, kcols] = dk.astype(jnp.bfloat16)
            low_ref[:, vcols] = dv.astype(jnp.bfloat16)
            own_ref[:, kcols] = dk[:tok_rows]
            own_ref[:, vcols] = dv[:tok_rows]

    return pl.pallas_call(
        kernel,
        out_shape=(
            jax.ShapeDtypeStruct((seq_rows, 2 * kv_cols), jnp.bfloat16),
            jax.ShapeDtypeStruct((tok_rows, 2 * kv_cols), jnp.float32),
        ),
    )(q3, g3, *kv_blocks, lower, upper)


def per_device(inputs, query, grad_out, w_key, w_value, keep_mask):
    tok_rows = inputs.shape[1]
    local_heads = query.shape[2]
    head_dim = query.shape[3]
    kv_cols = w_key.shape[2]
    kv_local = kv_cols // head_dim
    group_size = local_heads // kv_local
    scaling = 1.0 / math.sqrt(head_dim)
    ctx_len = lax.axis_size("ctx")
    ctx_index = lax.axis_index("ctx")
    tokens = inputs[0]
    key_rows = jnp.dot(tokens, w_key[0], preferred_element_type=jnp.float32).astype(jnp.bfloat16)
    value_rows = jnp.dot(tokens, w_value[0], preferred_element_type=jnp.float32).astype(
        jnp.bfloat16
    )
    kv_own = jnp.concatenate((key_rows, value_rows), axis=1)
    blocks = [kv_own] + [shifted(kv_own, "ctx", d, ctx_len, True) for d in range(1, ctx_len)]
    seq_rows = tok_rows * ctx_len
    first_row = ctx_index * tok_rows
    blk = jnp.arange(ctx_len, dtype=jnp.int32)
    col_pos = (
        (ctx_index - blk)[:, None] * tok_rows + jnp.arange(tok_rows, dtype=jnp.int32)[None, :]
    ).reshape(seq_rows, 1)
    keep_blocks = keep_mask.reshape(ctx_len, tok_rows)
    kept = jnp.concatenate(
        [
            lax.dynamic_index_in_dim(keep_blocks, jnp.maximum(ctx_index - p, 0), 0, keepdims=False)
            for p in range(ctx_len)
        ],
        axis=0,
    ).reshape(seq_rows, 1)
    never = jnp.iinfo(jnp.int32).max
    lower = jnp.where(col_pos >= 0, col_pos - first_row, never)
    upper = jnp.where(kept == 1, never, col_pos - first_row)
    q3 = jnp.transpose(query[0], (1, 0, 2))
    g3 = jnp.transpose(grad_out[0], (1, 0, 2))
    terms_low, kv_grad = attention_terms(
        q3, g3, blocks, lower, upper, kv_local, head_dim, scaling
    )
    for d in range(1, ctx_len):
        part = terms_low[d * tok_rows : (d + 1) * tok_rows]
        kv_grad = kv_grad + shifted(part, "ctx", d, ctx_len, False).astype(jnp.float32)
    grad_key = kv_grad[:, :kv_cols].astype(jnp.bfloat16)
    grad_value = kv_grad[:, kv_cols:].astype(jnp.bfloat16)
    contract = (((1,), (1,)), ((), ()))
    head_len = lax.axis_size("head")
    head_index = lax.axis_index("head")
    out_cols = w_key.shape[1] // head_len

    def partial_for(b):
        start = b * out_cols
        wk = lax.dynamic_slice_in_dim(w_key[0], start, out_cols, axis=0)
        wv = lax.dynamic_slice_in_dim(w_value[0], start, out_cols, axis=0)
        part = lax.dot_general(grad_key, wk, contract, preferred_element_type=jnp.float32)
        return part + lax.dot_general(grad_value, wv, contract, preferred_element_type=jnp.float32)

    received = []
    for d in range(1, head_len):
        target = lax.rem(head_index + d, head_len)
        send = partial_for(target).astype(jnp.bfloat16)
        perm = [(h, (h + d) % head_len) for h in range(head_len)]
        received.append(lax.ppermute(send, "head", perm))
    reduced = partial_for(head_index)
    for got in received:
        reduced = reduced + got.astype(jnp.float32)
    result = suffix_pipeline(reduced, "segment", CHAIN_CHUNKS)
    return result[None]


def solution(mesh):
    return jax.shard_map(
        per_device,
        mesh=mesh,
        in_specs=(
            P("segment", "ctx", None),
            P("segment", "ctx", "head", None),
            P("segment", "ctx", "head", None),
            P("segment", None, "head"),
            P("segment", None, "head"),
            P(),
        ),
        out_specs=P("segment", "ctx", "head"),
        check_vma=False,
    )
```

```python
import math

import jax
import jax.numpy as jnp
from jax import lax
from jax.experimental import pallas as pl
from jax.sharding import PartitionSpec as P


CHAIN_CHUNKS = 2


def shifted(x, axis, d, length, up):
    if up:
        perm = [(c, c + d) for c in range(length - d)]
    else:
        perm = [(c, c - d) for c in range(d, length)]
    return lax.ppermute(x, axis, perm)


def suffix_pipeline(chunks, axis):
    length, index = (lax.axis_size(axis), lax.axis_index(axis))
    n_chunks = len(chunks)
    height, cols = chunks[0].shape
    steps = n_chunks + length - 1
    recv = jnp.zeros((height, cols), jnp.bfloat16)
    done = []
    for tau in range(steps):
        which = tau - (length - 1 - index)
        own = jnp.zeros((height, cols), jnp.float32)
        for k in range(max(0, tau - length + 1), min(tau, n_chunks - 1) + 1):
            own = jnp.where(which == k, chunks[k], own)
        acc = own + recv.astype(jnp.float32)
        done.append(acc)
        perm = [(i, i - 1) for i in range(1, length) if 0 <= tau - (length - 1 - i) < n_chunks]
        if perm:
            recv = lax.ppermute(acc.astype(jnp.bfloat16), axis, perm)
    stacked = jnp.stack(done, axis=0)
    mine = lax.dynamic_slice_in_dim(stacked, length - 1 - index, n_chunks, axis=0)
    return mine.reshape(n_chunks * height, cols)


def attention_terms(q3, g3, kv_blocks, lower, upper, kv_local, head_dim, scaling):
    tok_rows = q3.shape[1]
    group = q3.shape[0] // kv_local
    n_blocks = len(kv_blocks)
    seq_rows = tok_rows * n_blocks
    kv_cols = kv_local * head_dim
    nt = (((1,), (1,)), ((), ()))

    def kernel(*refs):
        q_ref, g_ref = refs[0], refs[1]
        kv_refs = refs[2 : 2 + n_blocks]
        lo_ref, hi_ref, low_ref, own_ref = refs[2 + n_blocks :]
        rows = lax.broadcasted_iota(jnp.int32, (seq_rows, tok_rows), 1)
        allowed = (lo_ref[...] <= rows) & (rows <= hi_ref[...])
        for k in range(kv_local):
            kcols = slice(k * head_dim, (k + 1) * head_dim)
            vcols = slice(kv_cols + k * head_dim, kv_cols + (k + 1) * head_dim)
            key = jnp.concatenate([r[:, kcols] for r in kv_refs], axis=0)
            val = jnp.concatenate([r[:, vcols] for r in kv_refs], axis=0)
            dk = jnp.zeros((seq_rows, head_dim), jnp.float32)
            dv = jnp.zeros((seq_rows, head_dim), jnp.float32)
            for j in range(group):
                h = k * group + j
                q = q_ref[h]
                gr = g_ref[h]
                s = lax.dot_general(key, q, nt, preferred_element_type=jnp.float32) * scaling
                masked = jnp.where(allowed, s, -1e30)
                top = jnp.max(masked, axis=0, keepdims=True)
                tot = jnp.sum(jnp.where(allowed, jnp.exp(masked - top), 0.0), axis=0, keepdims=True)
                log_total = top + jnp.log(tot)
                p = jnp.where(allowed, jnp.exp(masked - log_total), 0.0)
                pb = p.astype(jnp.bfloat16)
                dp = lax.dot_general(val, gr, nt, preferred_element_type=jnp.float32)
                rd = jnp.sum(pb.astype(jnp.float32) * dp, axis=0, keepdims=True)
                ds = (p * (dp - rd)).astype(jnp.bfloat16)
                dv = dv + jnp.dot(pb, gr, preferred_element_type=jnp.float32)
                dk = dk + jnp.dot(ds, q, preferred_element_type=jnp.float32)
            dk = dk * scaling
            low_ref[:, kcols] = dk.astype(jnp.bfloat16)
            low_ref[:, vcols] = dv.astype(jnp.bfloat16)
            own_ref[:, kcols] = dk[:tok_rows]
            own_ref[:, vcols] = dv[:tok_rows]

    return pl.pallas_call(
        kernel,
        out_shape=(
            jax.ShapeDtypeStruct((seq_rows, 2 * kv_cols), jnp.bfloat16),
            jax.ShapeDtypeStruct((tok_rows, 2 * kv_cols), jnp.float32),
        ),
    )(q3, g3, *kv_blocks, lower, upper)


def per_device(inputs, query, grad_out, w_key, w_value, keep_mask):
    tok_rows = inputs.shape[1]
    local_heads = query.shape[2]
    head_dim = query.shape[3]
    kv_cols = w_key.shape[2]
    kv_local = kv_cols // head_dim
    group_size = local_heads // kv_local
    scaling = 1.0 / math.sqrt(head_dim)
    ctx_len = lax.axis_size("ctx")
    ctx_index = lax.axis_index("ctx")
    tokens = inputs[0]
    key_rows = jnp.dot(tokens, w_key[0], preferred_element_type=jnp.float32).astype(jnp.bfloat16)
    value_rows = jnp.dot(tokens, w_value[0], preferred_element_type=jnp.float32).astype(
        jnp.bfloat16
    )
    kv_own = jnp.concatenate((key_rows, value_rows), axis=1)
    blocks = [kv_own] + [shifted(kv_own, "ctx", d, ctx_len, True) for d in range(1, ctx_len)]
    seq_rows = tok_rows * ctx_len
    first_row = ctx_index * tok_rows
    blk = jnp.arange(ctx_len, dtype=jnp.int32)
    col_pos = (
        (ctx_index - blk)[:, None] * tok_rows + jnp.arange(tok_rows, dtype=jnp.int32)[None, :]
    ).reshape(seq_rows, 1)
    keep_blocks = keep_mask.reshape(ctx_len, tok_rows)
    kept = jnp.concatenate(
        [
            lax.dynamic_index_in_dim(keep_blocks, jnp.maximum(ctx_index - p, 0), 0, keepdims=False)
            for p in range(ctx_len)
        ],
        axis=0,
    ).reshape(seq_rows, 1)
    never = jnp.iinfo(jnp.int32).max
    lower = jnp.where(col_pos >= 0, col_pos - first_row, never)
    upper = jnp.where(kept == 1, never, col_pos - first_row)
    q3 = jnp.transpose(query[0], (1, 0, 2))
    g3 = jnp.transpose(grad_out[0], (1, 0, 2))
    terms_low, kv_grad = attention_terms(
        q3, g3, blocks, lower, upper, kv_local, head_dim, scaling
    )
    contract = (((1,), (1,)), ((), ()))
    head_len = lax.axis_size("head")
    head_index = lax.axis_index("head")
    out_cols = w_key.shape[1] // head_len
    height = tok_rows // CHAIN_CHUNKS

    def partial_for(b, grad_key, grad_value):
        start = b * out_cols
        wk = lax.dynamic_slice_in_dim(w_key[0], start, out_cols, axis=0)
        wv = lax.dynamic_slice_in_dim(w_value[0], start, out_cols, axis=0)
        part = lax.dot_general(grad_key, wk, contract, preferred_element_type=jnp.float32)
        return part + lax.dot_general(grad_value, wv, contract, preferred_element_type=jnp.float32)

    chunks = []
    for c in range(CHAIN_CHUNKS):
        lo_row = c * height
        chunk_grad = kv_grad[lo_row : lo_row + height]
        for d in range(1, ctx_len):
            part = terms_low[d * tok_rows + lo_row : d * tok_rows + lo_row + height]
            chunk_grad = chunk_grad + shifted(part, "ctx", d, ctx_len, False).astype(jnp.float32)
        grad_key = chunk_grad[:, :kv_cols].astype(jnp.bfloat16)
        grad_value = chunk_grad[:, kv_cols:].astype(jnp.bfloat16)
        received = []
        for d in range(1, head_len):
            target = lax.rem(head_index + d, head_len)
            send = partial_for(target, grad_key, grad_value).astype(jnp.bfloat16)
            perm = [(h, (h + d) % head_len) for h in range(head_len)]
            received.append(lax.ppermute(send, "head", perm))
        reduced = partial_for(head_index, grad_key, grad_value)
        for got in received:
            reduced = reduced + got.astype(jnp.float32)
        chunks.append(reduced)
    result = suffix_pipeline(chunks, "segment")
    return result[None]


def solution(mesh):
    return jax.shard_map(
        per_device,
        mesh=mesh,
        in_specs=(
            P("segment", "ctx", None),
            P("segment", "ctx", "head", None),
            P("segment", "ctx", "head", None),
            P("segment", None, "head"),
            P("segment", None, "head"),
            P(),
        ),
        out_specs=P("segment", "ctx", "head"),
        check_vma=False,
    )
```

```python
import math

import jax
import jax.numpy as jnp
from jax import lax
from jax.experimental import pallas as pl
from jax.sharding import PartitionSpec as P


CHAIN_CHUNKS = 2


def shifted(x, axis, d, length, up):
    if up:
        perm = [(c, c + d) for c in range(length - d)]
    else:
        perm = [(c, c - d) for c in range(d, length)]
    return lax.ppermute(x, axis, perm)


def suffix_pipeline(own, axis, n_chunks):
    length, index = (lax.axis_size(axis), lax.axis_index(axis))
    rows, cols = own.shape
    height = rows // n_chunks
    chunks = own.reshape(n_chunks, height, cols)
    pad = jnp.zeros((length - 1, height, cols), own.dtype)
    padded = jnp.concatenate((pad, chunks, pad), axis=0)
    steps = n_chunks + length - 1
    ordered = lax.dynamic_slice_in_dim(padded, index, steps, axis=0)
    recv = jnp.zeros((height, cols), jnp.bfloat16)
    done = []
    for tau in range(steps):
        acc = ordered[tau] + recv.astype(jnp.float32)
        done.append(acc)
        perm = [(i, i - 1) for i in range(1, length) if 0 <= tau - (length - 1 - i) < n_chunks]
        if perm:
            recv = lax.ppermute(acc.astype(jnp.bfloat16), axis, perm)
    stacked = jnp.stack(done, axis=0)
    mine = lax.dynamic_slice_in_dim(stacked, length - 1 - index, n_chunks, axis=0)
    return mine.reshape(rows, cols)


def attention_terms(q3, g3, kv_blocks, lower, upper, kv_local, head_dim, scaling):
    tok_rows = q3.shape[1]
    group = q3.shape[0] // kv_local
    n_blocks = len(kv_blocks)
    seq_rows = tok_rows * n_blocks
    kv_cols = kv_local * head_dim
    nt = (((1,), (1,)), ((), ()))

    def kernel(*refs):
        q_ref, g_ref = refs[0], refs[1]
        kv_refs = refs[2 : 2 + n_blocks]
        lo_ref, hi_ref, low_ref, own_ref = refs[2 + n_blocks :]
        rows = lax.broadcasted_iota(jnp.int32, (seq_rows, tok_rows), 1)
        allowed = (lo_ref[...] <= rows) & (rows <= hi_ref[...])
        for k in range(kv_local):
            kcols = slice(k * head_dim, (k + 1) * head_dim)
            vcols = slice(kv_cols + k * head_dim, kv_cols + (k + 1) * head_dim)
            key = jnp.concatenate([r[:, kcols] for r in kv_refs], axis=0)
            val = jnp.concatenate([r[:, vcols] for r in kv_refs], axis=0)
            dk = jnp.zeros((seq_rows, head_dim), jnp.float32)
            dv = jnp.zeros((seq_rows, head_dim), jnp.float32)
            for j in range(group):
                h = k * group + j
                q = q_ref[h]
                gr = g_ref[h]
                s = lax.dot_general(key, q, nt, preferred_element_type=jnp.float32) * scaling
                masked = jnp.where(allowed, s, -1e30)
                top = jnp.max(masked, axis=0, keepdims=True)
                tot = jnp.sum(jnp.where(allowed, jnp.exp(masked - top), 0.0), axis=0, keepdims=True)
                log_total = top + jnp.log(tot)
                p = jnp.where(allowed, jnp.exp(masked - log_total), 0.0)
                pb = p.astype(jnp.bfloat16)
                dp = lax.dot_general(val, gr, nt, preferred_element_type=jnp.float32)
                rd = jnp.sum(pb.astype(jnp.float32) * dp, axis=0, keepdims=True)
                ds = (p * (dp - rd)).astype(jnp.bfloat16)
                dv = dv + jnp.dot(pb, gr, preferred_element_type=jnp.float32)
                dk = dk + jnp.dot(ds, q, preferred_element_type=jnp.float32)
            dk = dk * scaling
            low_ref[:, kcols] = dk.astype(jnp.bfloat16)
            low_ref[:, vcols] = dv.astype(jnp.bfloat16)
            own_ref[:, kcols] = dk[:tok_rows]
            own_ref[:, vcols] = dv[:tok_rows]

    return pl.pallas_call(
        kernel,
        out_shape=(
            jax.ShapeDtypeStruct((seq_rows, 2 * kv_cols), jnp.bfloat16),
            jax.ShapeDtypeStruct((tok_rows, 2 * kv_cols), jnp.float32),
        ),
    )(q3, g3, *kv_blocks, lower, upper)


def per_device(inputs, query, grad_out, w_key, w_value, keep_mask):
    tok_rows = inputs.shape[1]
    local_heads = query.shape[2]
    head_dim = query.shape[3]
    kv_cols = w_key.shape[2]
    kv_local = kv_cols // head_dim
    group_size = local_heads // kv_local
    scaling = 1.0 / math.sqrt(head_dim)
    ctx_len = lax.axis_size("ctx")
    ctx_index = lax.axis_index("ctx")
    tokens = inputs[0]
    key_rows = jnp.dot(tokens, w_key[0], preferred_element_type=jnp.float32).astype(jnp.bfloat16)
    value_rows = jnp.dot(tokens, w_value[0], preferred_element_type=jnp.float32).astype(
        jnp.bfloat16
    )
    kv_own = jnp.concatenate((key_rows, value_rows), axis=1)
    blocks = [kv_own] + [shifted(kv_own, "ctx", d, ctx_len, True) for d in range(1, ctx_len)]
    seq_rows = tok_rows * ctx_len
    first_row = ctx_index * tok_rows
    blk = jnp.arange(ctx_len, dtype=jnp.int32)
    col_pos = (
        (ctx_index - blk)[:, None] * tok_rows + jnp.arange(tok_rows, dtype=jnp.int32)[None, :]
    ).reshape(seq_rows, 1)
    keep_blocks = keep_mask.reshape(ctx_len, tok_rows)
    kept = jnp.concatenate(
        [
            lax.dynamic_index_in_dim(keep_blocks, jnp.maximum(ctx_index - p, 0), 0, keepdims=False)
            for p in range(ctx_len)
        ],
        axis=0,
    ).reshape(seq_rows, 1)
    never = jnp.iinfo(jnp.int32).max
    lower = jnp.where(col_pos >= 0, col_pos - first_row, never)
    upper = jnp.where(kept == 1, never, col_pos - first_row)
    q3 = jnp.transpose(query[0], (1, 0, 2))
    g3 = jnp.transpose(grad_out[0], (1, 0, 2))
    terms_low, kv_grad = attention_terms(
        q3, g3, blocks, lower, upper, kv_local, head_dim, scaling
    )
    low_blocks = terms_low.reshape(ctx_len, tok_rows, terms_low.shape[1])
    targets = jnp.arange(ctx_len, dtype=jnp.int32)
    pick = ctx_index - targets
    outgoing = jnp.take(low_blocks, jnp.clip(pick, 0, ctx_len - 1), axis=0)
    outgoing = jnp.where(((pick >= 1))[:, None, None], outgoing, jnp.zeros_like(outgoing))
    incoming = lax.all_to_all(outgoing, "ctx", 0, 0, tiled=True)
    kv_grad = kv_grad + jnp.sum(incoming.astype(jnp.float32), axis=0)
    grad_key = kv_grad[:, :kv_cols].astype(jnp.bfloat16)
    grad_value = kv_grad[:, kv_cols:].astype(jnp.bfloat16)
    contract = (((1,), (1,)), ((), ()))
    head_len = lax.axis_size("head")
    head_index = lax.axis_index("head")
    out_cols = w_key.shape[1] // head_len

    def partial_for(b):
        start = b * out_cols
        wk = lax.dynamic_slice_in_dim(w_key[0], start, out_cols, axis=0)
        wv = lax.dynamic_slice_in_dim(w_value[0], start, out_cols, axis=0)
        part = lax.dot_general(grad_key, wk, contract, preferred_element_type=jnp.float32)
        return part + lax.dot_general(grad_value, wv, contract, preferred_element_type=jnp.float32)

    received = []
    for d in range(1, head_len):
        target = lax.rem(head_index + d, head_len)
        send = partial_for(target).astype(jnp.bfloat16)
        perm = [(h, (h + d) % head_len) for h in range(head_len)]
        received.append(lax.ppermute(send, "head", perm))
    reduced = partial_for(head_index)
    for got in received:
        reduced = reduced + got.astype(jnp.float32)
    result = suffix_pipeline(reduced, "segment", CHAIN_CHUNKS)
    return result[None]


def solution(mesh):
    return jax.shard_map(
        per_device,
        mesh=mesh,
        in_specs=(
            P("segment", "ctx", None),
            P("segment", "ctx", "head", None),
            P("segment", "ctx", "head", None),
            P("segment", None, "head"),
            P("segment", None, "head"),
            P(),
        ),
        out_specs=P("segment", "ctx", "head"),
        check_vma=False,
    )
```

```python
import math

import jax
import jax.numpy as jnp
from jax import lax
from jax.experimental import pallas as pl
from jax.sharding import PartitionSpec as P


CHAIN_CHUNKS = 4


def shifted(x, axis, d, length, up):
    if up:
        perm = [(c, c + d) for c in range(length - d)]
    else:
        perm = [(c, c - d) for c in range(d, length)]
    return lax.ppermute(x, axis, perm)


def suffix_pipeline(own, axis, n_chunks):
    length, index = (lax.axis_size(axis), lax.axis_index(axis))
    rows, cols = own.shape
    height = rows // n_chunks
    chunks = own.reshape(n_chunks, height, cols)
    partial = [chunks[k] for k in range(n_chunks)]
    history = [[chunks[k]] for k in range(n_chunks)]
    for hop in range(1, length):
        for k in range(n_chunks):
            sender = length - hop
            got = lax.ppermute(partial[k].astype(jnp.bfloat16), axis, [(sender, sender - 1)])
            partial[k] = chunks[k] + got.astype(jnp.float32)
            history[k].append(partial[k])
    out = [
        lax.dynamic_index_in_dim(jnp.stack(history[k], axis=0), length - 1 - index, 0, keepdims=False)
        for k in range(n_chunks)
    ]
    return jnp.concatenate(out, axis=0)


def attention_terms(q3, g3, kv_blocks, lower, upper, kv_local, head_dim, scaling):
    tok_rows = q3.shape[1]
    group = q3.shape[0] // kv_local
    n_blocks = len(kv_blocks)
    seq_rows = tok_rows * n_blocks
    kv_cols = kv_local * head_dim
    nt = (((1,), (1,)), ((), ()))

    def kernel(*refs):
        q_ref, g_ref = refs[0], refs[1]
        kv_refs = refs[2 : 2 + n_blocks]
        lo_ref, hi_ref, low_ref, own_ref = refs[2 + n_blocks :]
        rows = lax.broadcasted_iota(jnp.int32, (seq_rows, tok_rows), 1)
        allowed = (lo_ref[...] <= rows) & (rows <= hi_ref[...])
        for k in range(kv_local):
            kcols = slice(k * head_dim, (k + 1) * head_dim)
            vcols = slice(kv_cols + k * head_dim, kv_cols + (k + 1) * head_dim)
            key = jnp.concatenate([r[:, kcols] for r in kv_refs], axis=0)
            val = jnp.concatenate([r[:, vcols] for r in kv_refs], axis=0)
            dk = jnp.zeros((seq_rows, head_dim), jnp.float32)
            dv = jnp.zeros((seq_rows, head_dim), jnp.float32)
            for j in range(group):
                h = k * group + j
                q = q_ref[h]
                gr = g_ref[h]
                s = lax.dot_general(key, q, nt, preferred_element_type=jnp.float32) * scaling
                masked = jnp.where(allowed, s, -1e30)
                top = jnp.max(masked, axis=0, keepdims=True)
                tot = jnp.sum(jnp.where(allowed, jnp.exp(masked - top), 0.0), axis=0, keepdims=True)
                log_total = top + jnp.log(tot)
                p = jnp.where(allowed, jnp.exp(masked - log_total), 0.0)
                pb = p.astype(jnp.bfloat16)
                dp = lax.dot_general(val, gr, nt, preferred_element_type=jnp.float32)
                rd = jnp.sum(pb.astype(jnp.float32) * dp, axis=0, keepdims=True)
                ds = (p * (dp - rd)).astype(jnp.bfloat16)
                dv = dv + jnp.dot(pb, gr, preferred_element_type=jnp.float32)
                dk = dk + jnp.dot(ds, q, preferred_element_type=jnp.float32)
            dk = dk * scaling
            low_ref[:, kcols] = dk.astype(jnp.bfloat16)
            low_ref[:, vcols] = dv.astype(jnp.bfloat16)
            own_ref[:, kcols] = dk[:tok_rows]
            own_ref[:, vcols] = dv[:tok_rows]

    return pl.pallas_call(
        kernel,
        out_shape=(
            jax.ShapeDtypeStruct((seq_rows, 2 * kv_cols), jnp.bfloat16),
            jax.ShapeDtypeStruct((tok_rows, 2 * kv_cols), jnp.float32),
        ),
    )(q3, g3, *kv_blocks, lower, upper)


def per_device(inputs, query, grad_out, w_key, w_value, keep_mask):
    tok_rows = inputs.shape[1]
    local_heads = query.shape[2]
    head_dim = query.shape[3]
    kv_cols = w_key.shape[2]
    kv_local = kv_cols // head_dim
    group_size = local_heads // kv_local
    scaling = 1.0 / math.sqrt(head_dim)
    ctx_len = lax.axis_size("ctx")
    ctx_index = lax.axis_index("ctx")
    tokens = inputs[0]
    key_rows = jnp.dot(tokens, w_key[0], preferred_element_type=jnp.float32).astype(jnp.bfloat16)
    value_rows = jnp.dot(tokens, w_value[0], preferred_element_type=jnp.float32).astype(
        jnp.bfloat16
    )
    kv_own = jnp.concatenate((key_rows, value_rows), axis=1)
    blocks = [kv_own] + [shifted(kv_own, "ctx", d, ctx_len, True) for d in range(1, ctx_len)]
    seq_rows = tok_rows * ctx_len
    first_row = ctx_index * tok_rows
    blk = jnp.arange(ctx_len, dtype=jnp.int32)
    col_pos = (
        (ctx_index - blk)[:, None] * tok_rows + jnp.arange(tok_rows, dtype=jnp.int32)[None, :]
    ).reshape(seq_rows, 1)
    keep_blocks = keep_mask.reshape(ctx_len, tok_rows)
    kept = jnp.concatenate(
        [
            lax.dynamic_index_in_dim(keep_blocks, jnp.maximum(ctx_index - p, 0), 0, keepdims=False)
            for p in range(ctx_len)
        ],
        axis=0,
    ).reshape(seq_rows, 1)
    never = jnp.iinfo(jnp.int32).max
    lower = jnp.where(col_pos >= 0, col_pos - first_row, never)
    upper = jnp.where(kept == 1, never, col_pos - first_row)
    q3 = jnp.transpose(query[0], (1, 0, 2))
    g3 = jnp.transpose(grad_out[0], (1, 0, 2))
    terms_low, kv_grad = attention_terms(
        q3, g3, blocks, lower, upper, kv_local, head_dim, scaling
    )
    for d in range(1, ctx_len):
        part = terms_low[d * tok_rows : (d + 1) * tok_rows]
        kv_grad = kv_grad + shifted(part, "ctx", d, ctx_len, False).astype(jnp.float32)
    grad_key = kv_grad[:, :kv_cols].astype(jnp.bfloat16)
    grad_value = kv_grad[:, kv_cols:].astype(jnp.bfloat16)
    contract = (((1,), (1,)), ((), ()))
    head_len = lax.axis_size("head")
    head_index = lax.axis_index("head")
    out_cols = w_key.shape[1] // head_len

    def partial_for(b):
        start = b * out_cols
        wk = lax.dynamic_slice_in_dim(w_key[0], start, out_cols, axis=0)
        wv = lax.dynamic_slice_in_dim(w_value[0], start, out_cols, axis=0)
        part = lax.dot_general(grad_key, wk, contract, preferred_element_type=jnp.float32)
        return part + lax.dot_general(grad_value, wv, contract, preferred_element_type=jnp.float32)

    received = []
    for d in range(1, head_len):
        target = lax.rem(head_index + d, head_len)
        send = partial_for(target).astype(jnp.bfloat16)
        perm = [(h, (h + d) % head_len) for h in range(head_len)]
        received.append(lax.ppermute(send, "head", perm))
    reduced = partial_for(head_index)
    for got in received:
        reduced = reduced + got.astype(jnp.float32)
    result = suffix_pipeline(reduced, "segment", CHAIN_CHUNKS)
    return result[None]


def solution(mesh):
    return jax.shard_map(
        per_device,
        mesh=mesh,
        in_specs=(
            P("segment", "ctx", None),
            P("segment", "ctx", "head", None),
            P("segment", "ctx", "head", None),
            P("segment", None, "head"),
            P("segment", None, "head"),
            P(),
        ),
        out_specs=P("segment", "ctx", "head"),
        check_vma=False,
    )
```

```python
import math

import jax
import jax.numpy as jnp
from jax import lax
from jax.experimental import pallas as pl
from jax.sharding import PartitionSpec as P


CHAIN_CHUNKS = 2


def shifted(x, axis, d, length, up):
    if up:
        perm = [(c, c + d) for c in range(length - d)]
    else:
        perm = [(c, c - d) for c in range(d, length)]
    return lax.ppermute(x, axis, perm)


def suffix_pipeline(own, axis, n_chunks):
    length, index = (lax.axis_size(axis), lax.axis_index(axis))
    rows, cols = own.shape
    height = rows // n_chunks
    chunks = own.reshape(n_chunks, height, cols)
    pad = jnp.zeros((length - 1, height, cols), own.dtype)
    padded = jnp.concatenate((pad, chunks, pad), axis=0)
    steps = n_chunks + length - 1
    ordered = lax.dynamic_slice_in_dim(padded, index, steps, axis=0)
    perm = [(i, i - 1) for i in range(1, length)]
    recv = jnp.zeros((height, cols), jnp.bfloat16)
    done = []
    for tau in range(steps):
        acc = ordered[tau] + recv.astype(jnp.float32)
        done.append(acc)
        if tau < steps - 1:
            recv = lax.ppermute(acc.astype(jnp.bfloat16), axis, perm)
    stacked = jnp.stack(done, axis=0)
    mine = lax.dynamic_slice_in_dim(stacked, length - 1 - index, n_chunks, axis=0)
    return mine.reshape(rows, cols)


def attention_terms(q3, g3, kv_blocks, lower, upper, kv_local, head_dim, scaling):
    tok_rows = q3.shape[1]
    group = q3.shape[0] // kv_local
    n_blocks = len(kv_blocks)
    seq_rows = tok_rows * n_blocks
    kv_cols = kv_local * head_dim
    nt = (((1,), (1,)), ((), ()))

    def kernel(*refs):
        q_ref, g_ref = refs[0], refs[1]
        kv_refs = refs[2 : 2 + n_blocks]
        lo_ref, hi_ref, low_ref, own_ref = refs[2 + n_blocks :]
        rows = lax.broadcasted_iota(jnp.int32, (seq_rows, tok_rows), 1)
        allowed = (lo_ref[...] <= rows) & (rows <= hi_ref[...])
        for k in range(kv_local):
            kcols = slice(k * head_dim, (k + 1) * head_dim)
            vcols = slice(kv_cols + k * head_dim, kv_cols + (k + 1) * head_dim)
            key = jnp.concatenate([r[:, kcols] for r in kv_refs], axis=0)
            val = jnp.concatenate([r[:, vcols] for r in kv_refs], axis=0)
            dk = jnp.zeros((seq_rows, head_dim), jnp.float32)
            dv = jnp.zeros((seq_rows, head_dim), jnp.float32)
            for j in range(group):
                h = k * group + j
                q = q_ref[h]
                gr = g_ref[h]
                s = lax.dot_general(key, q, nt, preferred_element_type=jnp.float32) * scaling
                masked = jnp.where(allowed, s, -1e30)
                top = jnp.max(masked, axis=0, keepdims=True)
                e = jnp.where(allowed, jnp.exp(masked - top), 0.0)
                tot = jnp.sum(e, axis=0, keepdims=True)
                p = e * (1.0 / tot)
                pb = p.astype(jnp.bfloat16)
                dp = lax.dot_general(val, gr, nt, preferred_element_type=jnp.float32)
                rd = jnp.sum(pb.astype(jnp.float32) * dp, axis=0, keepdims=True)
                ds = (p * (dp - rd)).astype(jnp.bfloat16)
                dv = dv + jnp.dot(pb, gr, preferred_element_type=jnp.float32)
                dk = dk + jnp.dot(ds, q, preferred_element_type=jnp.float32)
            dk = dk * scaling
            low_ref[:, kcols] = dk.astype(jnp.bfloat16)
            low_ref[:, vcols] = dv.astype(jnp.bfloat16)
            own_ref[:, kcols] = dk[:tok_rows]
            own_ref[:, vcols] = dv[:tok_rows]

    return pl.pallas_call(
        kernel,
        out_shape=(
            jax.ShapeDtypeStruct((seq_rows, 2 * kv_cols), jnp.bfloat16),
            jax.ShapeDtypeStruct((tok_rows, 2 * kv_cols), jnp.float32),
        ),
    )(q3, g3, *kv_blocks, lower, upper)


def per_device(inputs, query, grad_out, w_key, w_value, keep_mask):
    tok_rows = inputs.shape[1]
    local_heads = query.shape[2]
    head_dim = query.shape[3]
    kv_cols = w_key.shape[2]
    kv_local = kv_cols // head_dim
    group_size = local_heads // kv_local
    scaling = 1.0 / math.sqrt(head_dim)
    ctx_len = lax.axis_size("ctx")
    ctx_index = lax.axis_index("ctx")
    tokens = inputs[0]
    key_rows = jnp.dot(tokens, w_key[0], preferred_element_type=jnp.float32).astype(jnp.bfloat16)
    value_rows = jnp.dot(tokens, w_value[0], preferred_element_type=jnp.float32).astype(
        jnp.bfloat16
    )
    kv_own = jnp.concatenate((key_rows, value_rows), axis=1)
    later = {d: shifted(kv_own, "ctx", d, ctx_len, True) for d in range(ctx_len - 1, 0, -1)}
    blocks = [kv_own] + [later[d] for d in range(1, ctx_len)]
    seq_rows = tok_rows * ctx_len
    first_row = ctx_index * tok_rows
    blk = jnp.arange(ctx_len, dtype=jnp.int32)
    col_pos = (
        (ctx_index - blk)[:, None] * tok_rows + jnp.arange(tok_rows, dtype=jnp.int32)[None, :]
    ).reshape(seq_rows, 1)
    keep_blocks = keep_mask.reshape(ctx_len, tok_rows)
    kept = jnp.concatenate(
        [
            lax.dynamic_index_in_dim(keep_blocks, jnp.maximum(ctx_index - p, 0), 0, keepdims=False)
            for p in range(ctx_len)
        ],
        axis=0,
    ).reshape(seq_rows, 1)
    never = jnp.iinfo(jnp.int32).max
    lower = jnp.where(col_pos >= 0, col_pos - first_row, never)
    upper = jnp.where(kept == 1, never, col_pos - first_row)
    q3 = jnp.transpose(query[0], (1, 0, 2))
    g3 = jnp.transpose(grad_out[0], (1, 0, 2))
    terms_low, kv_grad = attention_terms(
        q3, g3, blocks, lower, upper, kv_local, head_dim, scaling
    )
    for d in range(1, ctx_len):
        part = terms_low[d * tok_rows : (d + 1) * tok_rows]
        kv_grad = kv_grad + shifted(part, "ctx", d, ctx_len, False).astype(jnp.float32)
    grad_key = kv_grad[:, :kv_cols].astype(jnp.bfloat16)
    grad_value = kv_grad[:, kv_cols:].astype(jnp.bfloat16)
    contract = (((1,), (1,)), ((), ()))
    head_len = lax.axis_size("head")
    head_index = lax.axis_index("head")
    out_cols = w_key.shape[1] // head_len

    def partial_for(b):
        start = b * out_cols
        wk = lax.dynamic_slice_in_dim(w_key[0], start, out_cols, axis=0)
        wv = lax.dynamic_slice_in_dim(w_value[0], start, out_cols, axis=0)
        part = lax.dot_general(grad_key, wk, contract, preferred_element_type=jnp.float32)
        return part + lax.dot_general(grad_value, wv, contract, preferred_element_type=jnp.float32)

    received = []
    for d in range(1, head_len):
        target = lax.rem(head_index + d, head_len)
        send = partial_for(target).astype(jnp.bfloat16)
        perm = [(h, (h + d) % head_len) for h in range(head_len)]
        received.append(lax.ppermute(send, "head", perm))
    reduced = partial_for(head_index)
    for got in received:
        reduced = reduced + got.astype(jnp.float32)
    result = suffix_pipeline(reduced, "segment", CHAIN_CHUNKS)
    return result[None]


def solution(mesh):
    return jax.shard_map(
        per_device,
        mesh=mesh,
        in_specs=(
            P("segment", "ctx", None),
            P("segment", "ctx", "head", None),
            P("segment", "ctx", "head", None),
            P("segment", None, "head"),
            P("segment", None, "head"),
            P(),
        ),
        out_specs=P("segment", "ctx", "head"),
        check_vma=False,
    )
```

```python
import math

import jax
import jax.numpy as jnp
from jax import lax
from jax.experimental import pallas as pl
from jax.sharding import PartitionSpec as P


CHAIN_CHUNKS = 4


def shifted(x, axis, d, length, up):
    if up:
        perm = [(c, c + d) for c in range(length - d)]
    else:
        perm = [(c, c - d) for c in range(d, length)]
    return lax.ppermute(x, axis, perm)


def suffix_pipeline(own, axis, n_chunks):
    length, index = (lax.axis_size(axis), lax.axis_index(axis))
    rows, cols = own.shape
    height = rows // n_chunks
    chunks = own.reshape(n_chunks, height, cols)
    pad = jnp.zeros((length - 1, height, cols), own.dtype)
    padded = jnp.concatenate((pad, chunks, pad), axis=0)
    steps = n_chunks + length - 1
    ordered = lax.dynamic_slice_in_dim(padded, index, steps, axis=0)
    recv = jnp.zeros((height, cols), jnp.bfloat16)
    done = []
    for tau in range(steps):
        acc = ordered[tau] + recv.astype(jnp.float32)
        done.append(acc)
        perm = [(i, i - 1) for i in range(1, length) if 0 <= tau - (length - 1 - i) < n_chunks]
        if perm:
            recv = lax.ppermute(acc.astype(jnp.bfloat16), axis, perm)
    stacked = jnp.stack(done, axis=0)
    mine = lax.dynamic_slice_in_dim(stacked, length - 1 - index, n_chunks, axis=0)
    return mine.reshape(rows, cols)


def attention_terms(q3, g3, kv_blocks, lower, upper, kv_local, head_dim, scaling):
    tok_rows = q3.shape[1]
    group = q3.shape[0] // kv_local
    n_blocks = len(kv_blocks)
    seq_rows = tok_rows * n_blocks
    kv_cols = kv_local * head_dim
    nt = (((1,), (1,)), ((), ()))

    def kernel(*refs):
        q_ref, g_ref = refs[0], refs[1]
        kv_refs = refs[2 : 2 + n_blocks]
        lo_ref, hi_ref, low_ref, own_ref = refs[2 + n_blocks :]
        rows = lax.broadcasted_iota(jnp.int32, (seq_rows, tok_rows), 1)
        allowed = (lo_ref[...] <= rows) & (rows <= hi_ref[...])
        for k in range(kv_local):
            kcols = slice(k * head_dim, (k + 1) * head_dim)
            vcols = slice(kv_cols + k * head_dim, kv_cols + (k + 1) * head_dim)
            key = jnp.concatenate([r[:, kcols] for r in kv_refs], axis=0)
            val = jnp.concatenate([r[:, vcols] for r in kv_refs], axis=0)
            dk = jnp.zeros((seq_rows, head_dim), jnp.float32)
            dv = jnp.zeros((seq_rows, head_dim), jnp.float32)
            for j in range(group):
                h = k * group + j
                q = q_ref[h]
                gr = g_ref[h]
                s = lax.dot_general(key, q, nt, preferred_element_type=jnp.float32) * scaling
                masked = jnp.where(allowed, s, -1e30)
                top = jnp.max(masked, axis=0, keepdims=True)
                e = jnp.where(allowed, jnp.exp(masked - top), 0.0)
                tot = jnp.sum(e, axis=0, keepdims=True)
                p = e * (1.0 / tot)
                pb = p.astype(jnp.bfloat16)
                dp = lax.dot_general(val, gr, nt, preferred_element_type=jnp.float32)
                rd = jnp.sum(pb.astype(jnp.float32) * dp, axis=0, keepdims=True)
                ds = (p * (dp - rd)).astype(jnp.bfloat16)
                dv = dv + jnp.dot(pb, gr, preferred_element_type=jnp.float32)
                dk = dk + jnp.dot(ds, q, preferred_element_type=jnp.float32)
            dk = dk * scaling
            low_ref[:, kcols] = dk.astype(jnp.bfloat16)
            low_ref[:, vcols] = dv.astype(jnp.bfloat16)
            own_ref[:, kcols] = dk[:tok_rows]
            own_ref[:, vcols] = dv[:tok_rows]

    return pl.pallas_call(
        kernel,
        out_shape=(
            jax.ShapeDtypeStruct((seq_rows, 2 * kv_cols), jnp.bfloat16),
            jax.ShapeDtypeStruct((tok_rows, 2 * kv_cols), jnp.float32),
        ),
    )(q3, g3, *kv_blocks, lower, upper)


def per_device(inputs, query, grad_out, w_key, w_value, keep_mask):
    tok_rows = inputs.shape[1]
    local_heads = query.shape[2]
    head_dim = query.shape[3]
    kv_cols = w_key.shape[2]
    kv_local = kv_cols // head_dim
    group_size = local_heads // kv_local
    scaling = 1.0 / math.sqrt(head_dim)
    ctx_len = lax.axis_size("ctx")
    ctx_index = lax.axis_index("ctx")
    tokens = inputs[0]
    key_rows = jnp.dot(tokens, w_key[0], preferred_element_type=jnp.float32).astype(jnp.bfloat16)
    value_rows = jnp.dot(tokens, w_value[0], preferred_element_type=jnp.float32).astype(
        jnp.bfloat16
    )
    kv_own = jnp.concatenate((key_rows, value_rows), axis=1)
    later = {d: shifted(kv_own, "ctx", d, ctx_len, True) for d in range(ctx_len - 1, 0, -1)}
    blocks = [kv_own] + [later[d] for d in range(1, ctx_len)]
    seq_rows = tok_rows * ctx_len
    first_row = ctx_index * tok_rows
    blk = jnp.arange(ctx_len, dtype=jnp.int32)
    col_pos = (
        (ctx_index - blk)[:, None] * tok_rows + jnp.arange(tok_rows, dtype=jnp.int32)[None, :]
    ).reshape(seq_rows, 1)
    keep_blocks = keep_mask.reshape(ctx_len, tok_rows)
    kept = jnp.concatenate(
        [
            lax.dynamic_index_in_dim(keep_blocks, jnp.maximum(ctx_index - p, 0), 0, keepdims=False)
            for p in range(ctx_len)
        ],
        axis=0,
    ).reshape(seq_rows, 1)
    never = jnp.iinfo(jnp.int32).max
    lower = jnp.where(col_pos >= 0, col_pos - first_row, never)
    upper = jnp.where(kept == 1, never, col_pos - first_row)
    q3 = jnp.transpose(query[0], (1, 0, 2))
    g3 = jnp.transpose(grad_out[0], (1, 0, 2))
    terms_low, kv_grad = attention_terms(
        q3, g3, blocks, lower, upper, kv_local, head_dim, scaling
    )
    for d in range(1, ctx_len):
        part = terms_low[d * tok_rows : (d + 1) * tok_rows]
        kv_grad = kv_grad + shifted(part, "ctx", d, ctx_len, False).astype(jnp.float32)
    grad_key = kv_grad[:, :kv_cols].astype(jnp.bfloat16)
    grad_value = kv_grad[:, kv_cols:].astype(jnp.bfloat16)
    contract = (((1,), (1,)), ((), ()))
    head_len = lax.axis_size("head")
    head_index = lax.axis_index("head")
    out_cols = w_key.shape[1] // head_len

    def partial_for(b):
        start = b * out_cols
        wk = lax.dynamic_slice_in_dim(w_key[0], start, out_cols, axis=0)
        wv = lax.dynamic_slice_in_dim(w_value[0], start, out_cols, axis=0)
        part = lax.dot_general(grad_key, wk, contract, preferred_element_type=jnp.float32)
        return part + lax.dot_general(grad_value, wv, contract, preferred_element_type=jnp.float32)

    received = []
    for d in range(1, head_len):
        target = lax.rem(head_index + d, head_len)
        send = partial_for(target).astype(jnp.bfloat16)
        perm = [(h, (h + d) % head_len) for h in range(head_len)]
        received.append(lax.ppermute(send, "head", perm))
    reduced = partial_for(head_index)
    for got in received:
        reduced = reduced + got.astype(jnp.float32)
    result = suffix_pipeline(reduced, "segment", CHAIN_CHUNKS)
    return result[None]


def solution(mesh):
    return jax.shard_map(
        per_device,
        mesh=mesh,
        in_specs=(
            P("segment", "ctx", None),
            P("segment", "ctx", "head", None),
            P("segment", "ctx", "head", None),
            P("segment", None, "head"),
            P("segment", None, "head"),
            P(),
        ),
        out_specs=P("segment", "ctx", "head"),
        check_vma=False,
    )
```

```python
import math

import jax
import jax.numpy as jnp
from jax import lax
from jax.experimental import pallas as pl
from jax.sharding import PartitionSpec as P


CHAIN_CHUNKS = 2


def shifted(x, axis, d, length, up):
    if up:
        perm = [(c, c + d) for c in range(length - d)]
    else:
        perm = [(c, c - d) for c in range(d, length)]
    return lax.ppermute(x, axis, perm)


def suffix_pipeline(own, axis, n_chunks):
    length, index = (lax.axis_size(axis), lax.axis_index(axis))
    rows, cols = own.shape
    height = rows // n_chunks
    chunks = own.reshape(n_chunks, height, cols)
    pad = jnp.zeros((length - 1, height, cols), own.dtype)
    padded = jnp.concatenate((pad, chunks, pad), axis=0)
    steps = n_chunks + length - 1
    ordered = lax.dynamic_slice_in_dim(padded, index, steps, axis=0)
    perm = [(i, i - 1) for i in range(1, length)]
    recv = jnp.zeros((height, cols), jnp.bfloat16)
    done = []
    for tau in range(steps):
        acc = ordered[tau] + recv.astype(jnp.float32)
        done.append(acc)
        if tau < steps - 1:
            recv = lax.ppermute(acc.astype(jnp.bfloat16), axis, perm)
    stacked = jnp.stack(done, axis=0)
    mine = lax.dynamic_slice_in_dim(stacked, length - 1 - index, n_chunks, axis=0)
    return mine.reshape(rows, cols)


def attention_terms(q3, g3, kv_blocks, lower, upper, kv_local, head_dim, scaling):
    tok_rows = q3.shape[1]
    group = q3.shape[0] // kv_local
    n_blocks = len(kv_blocks)
    seq_rows = tok_rows * n_blocks
    kv_cols = kv_local * head_dim
    nt = (((1,), (1,)), ((), ()))

    def kernel(*refs):
        q_ref, g_ref = refs[0], refs[1]
        kv_refs = refs[2 : 2 + n_blocks]
        lo_ref, hi_ref, own_ref = refs[2 + n_blocks : 5 + n_blocks]
        send_refs = refs[5 + n_blocks :]
        rows = lax.broadcasted_iota(jnp.int32, (seq_rows, tok_rows), 1)
        allowed = (lo_ref[...] <= rows) & (rows <= hi_ref[...])
        for k in range(kv_local):
            kcols = slice(k * head_dim, (k + 1) * head_dim)
            vcols = slice(kv_cols + k * head_dim, kv_cols + (k + 1) * head_dim)
            key = jnp.concatenate([r[:, kcols] for r in kv_refs], axis=0)
            val = jnp.concatenate([r[:, vcols] for r in kv_refs], axis=0)
            dk = jnp.zeros((seq_rows, head_dim), jnp.float32)
            dv = jnp.zeros((seq_rows, head_dim), jnp.float32)
            for j in range(group):
                h = k * group + j
                q = q_ref[h]
                gr = g_ref[h]
                s = lax.dot_general(key, q, nt, preferred_element_type=jnp.float32) * scaling
                masked = jnp.where(allowed, s, -1e30)
                top = jnp.max(masked, axis=0, keepdims=True)
                e = jnp.where(allowed, jnp.exp(masked - top), 0.0)
                tot = jnp.sum(e, axis=0, keepdims=True)
                p = e * (1.0 / tot)
                pb = p.astype(jnp.bfloat16)
                dp = lax.dot_general(val, gr, nt, preferred_element_type=jnp.float32)
                rd = jnp.sum(pb.astype(jnp.float32) * dp, axis=0, keepdims=True)
                ds = (p * (dp - rd)).astype(jnp.bfloat16)
                dv = dv + jnp.dot(pb, gr, preferred_element_type=jnp.float32)
                dk = dk + jnp.dot(ds, q, preferred_element_type=jnp.float32)
            dk = dk * scaling
            own_ref[:, kcols] = dk[:tok_rows]
            own_ref[:, vcols] = dv[:tok_rows]
            for p, send_ref in enumerate(send_refs, start=1):
                send_ref[:, kcols] = dk[p * tok_rows : (p + 1) * tok_rows].astype(jnp.bfloat16)
                send_ref[:, vcols] = dv[p * tok_rows : (p + 1) * tok_rows].astype(jnp.bfloat16)

    return pl.pallas_call(
        kernel,
        out_shape=(jax.ShapeDtypeStruct((tok_rows, 2 * kv_cols), jnp.float32),)
        + tuple(
            jax.ShapeDtypeStruct((tok_rows, 2 * kv_cols), jnp.bfloat16) for _ in range(n_blocks - 1)
        ),
    )(q3, g3, *kv_blocks, lower, upper)


def per_device(inputs, query, grad_out, w_key, w_value, keep_mask):
    tok_rows = inputs.shape[1]
    local_heads = query.shape[2]
    head_dim = query.shape[3]
    kv_cols = w_key.shape[2]
    kv_local = kv_cols // head_dim
    group_size = local_heads // kv_local
    scaling = 1.0 / math.sqrt(head_dim)
    ctx_len = lax.axis_size("ctx")
    ctx_index = lax.axis_index("ctx")
    tokens = inputs[0]
    key_rows = jnp.dot(tokens, w_key[0], preferred_element_type=jnp.float32).astype(jnp.bfloat16)
    value_rows = jnp.dot(tokens, w_value[0], preferred_element_type=jnp.float32).astype(
        jnp.bfloat16
    )
    kv_own = jnp.concatenate((key_rows, value_rows), axis=1)
    later = {d: shifted(kv_own, "ctx", d, ctx_len, True) for d in range(ctx_len - 1, 0, -1)}
    blocks = [kv_own] + [later[d] for d in range(1, ctx_len)]
    seq_rows = tok_rows * ctx_len
    first_row = ctx_index * tok_rows
    blk = jnp.arange(ctx_len, dtype=jnp.int32)
    col_pos = (
        (ctx_index - blk)[:, None] * tok_rows + jnp.arange(tok_rows, dtype=jnp.int32)[None, :]
    ).reshape(seq_rows, 1)
    keep_blocks = keep_mask.reshape(ctx_len, tok_rows)
    kept = jnp.concatenate(
        [
            lax.dynamic_index_in_dim(keep_blocks, jnp.maximum(ctx_index - p, 0), 0, keepdims=False)
            for p in range(ctx_len)
        ],
        axis=0,
    ).reshape(seq_rows, 1)
    never = jnp.iinfo(jnp.int32).max
    lower = jnp.where(col_pos >= 0, col_pos - first_row, never)
    upper = jnp.where(kept == 1, never, col_pos - first_row)
    q3 = jnp.transpose(query[0], (1, 0, 2))
    g3 = jnp.transpose(grad_out[0], (1, 0, 2))
    kv_grad, *parts = attention_terms(q3, g3, blocks, lower, upper, kv_local, head_dim, scaling)
    for d in range(1, ctx_len):
        part = parts[d - 1]
        kv_grad = kv_grad + shifted(part, "ctx", d, ctx_len, False).astype(jnp.float32)
    grad_key = kv_grad[:, :kv_cols].astype(jnp.bfloat16)
    grad_value = kv_grad[:, kv_cols:].astype(jnp.bfloat16)
    contract = (((1,), (1,)), ((), ()))
    head_len = lax.axis_size("head")
    head_index = lax.axis_index("head")
    out_cols = w_key.shape[1] // head_len

    def partial_for(b):
        start = b * out_cols
        wk = lax.dynamic_slice_in_dim(w_key[0], start, out_cols, axis=0)
        wv = lax.dynamic_slice_in_dim(w_value[0], start, out_cols, axis=0)
        part = lax.dot_general(grad_key, wk, contract, preferred_element_type=jnp.float32)
        return part + lax.dot_general(grad_value, wv, contract, preferred_element_type=jnp.float32)

    received = []
    for d in range(1, head_len):
        target = lax.rem(head_index + d, head_len)
        send = partial_for(target).astype(jnp.bfloat16)
        perm = [(h, (h + d) % head_len) for h in range(head_len)]
        received.append(lax.ppermute(send, "head", perm))
    reduced = partial_for(head_index)
    for got in received:
        reduced = reduced + got.astype(jnp.float32)
    result = suffix_pipeline(reduced, "segment", CHAIN_CHUNKS)
    return result[None]


def solution(mesh):
    return jax.shard_map(
        per_device,
        mesh=mesh,
        in_specs=(
            P("segment", "ctx", None),
            P("segment", "ctx", "head", None),
            P("segment", "ctx", "head", None),
            P("segment", None, "head"),
            P("segment", None, "head"),
            P(),
        ),
        out_specs=P("segment", "ctx", "head"),
        check_vma=False,
    )
```

```python
import math

import jax
import jax.numpy as jnp
from jax import lax
from jax.experimental import pallas as pl
from jax.sharding import PartitionSpec as P


CHAIN_CHUNKS = 2


def shifted(x, axis, d, length, up):
    if up:
        perm = [(c, c + d) for c in range(length - d)]
    else:
        perm = [(c, c - d) for c in range(d, length)]
    return lax.ppermute(x, axis, perm)


def suffix_pipeline(own, axis, n_chunks):
    length, index = (lax.axis_size(axis), lax.axis_index(axis))
    rows, cols = own.shape
    height = rows // n_chunks
    chunks = own.reshape(n_chunks, height, cols)
    steps = n_chunks + length - 1
    recv = jnp.zeros((height, cols), jnp.bfloat16)
    out = jnp.zeros((n_chunks, height, cols), jnp.float32)
    for tau in range(steps):
        which = tau - (length - 1 - index)
        at = jnp.clip(which, 0, n_chunks - 1)
        acc = lax.dynamic_index_in_dim(chunks, at, 0, keepdims=False) + recv.astype(jnp.float32)
        perm = [(i, i - 1) for i in range(1, length) if 0 <= tau - (length - 1 - i) < n_chunks]
        if perm:
            recv = lax.ppermute(acc.astype(jnp.bfloat16), axis, perm)
        valid = (which >= 0) & (which < n_chunks)
        cur = lax.dynamic_index_in_dim(out, at, 0, keepdims=False)
        out = lax.dynamic_update_index_in_dim(out, jnp.where(valid, acc, cur), at, 0)
    return out.reshape(rows, cols)


def attention_terms(q3, g3, kv_blocks, lower, upper, kv_local, head_dim, scaling):
    tok_rows = q3.shape[1]
    group = q3.shape[0] // kv_local
    n_blocks = len(kv_blocks)
    seq_rows = tok_rows * n_blocks
    kv_cols = kv_local * head_dim
    nt = (((1,), (1,)), ((), ()))

    def kernel(*refs):
        q_ref, g_ref = refs[0], refs[1]
        kv_refs = refs[2 : 2 + n_blocks]
        lo_ref, hi_ref, own_ref = refs[2 + n_blocks : 5 + n_blocks]
        send_refs = refs[5 + n_blocks :]
        rows = lax.broadcasted_iota(jnp.int32, (seq_rows, tok_rows), 1)
        allowed = (lo_ref[...] <= rows) & (rows <= hi_ref[...])
        for k in range(kv_local):
            kcols = slice(k * head_dim, (k + 1) * head_dim)
            vcols = slice(kv_cols + k * head_dim, kv_cols + (k + 1) * head_dim)
            key = jnp.concatenate([r[:, kcols] for r in kv_refs], axis=0)
            val = jnp.concatenate([r[:, vcols] for r in kv_refs], axis=0)
            dk = jnp.zeros((seq_rows, head_dim), jnp.float32)
            dv = jnp.zeros((seq_rows, head_dim), jnp.float32)
            for j in range(group):
                h = k * group + j
                q = q_ref[h]
                gr = g_ref[h]
                s = lax.dot_general(key, q, nt, preferred_element_type=jnp.float32) * scaling
                masked = jnp.where(allowed, s, -1e30)
                top = jnp.max(masked, axis=0, keepdims=True)
                e = jnp.where(allowed, jnp.exp(masked - top), 0.0)
                tot = jnp.sum(e, axis=0, keepdims=True)
                p = e * (1.0 / tot)
                pb = p.astype(jnp.bfloat16)
                dp = lax.dot_general(val, gr, nt, preferred_element_type=jnp.float32)
                rd = jnp.sum(pb.astype(jnp.float32) * dp, axis=0, keepdims=True)
                ds = (p * (dp - rd)).astype(jnp.bfloat16)
                dv = dv + jnp.dot(pb, gr, preferred_element_type=jnp.float32)
                dk = dk + jnp.dot(ds, q, preferred_element_type=jnp.float32)
            dk = dk * scaling
            own_ref[:, kcols] = dk[:tok_rows]
            own_ref[:, vcols] = dv[:tok_rows]
            for p, send_ref in enumerate(send_refs, start=1):
                send_ref[:, kcols] = dk[p * tok_rows : (p + 1) * tok_rows].astype(jnp.bfloat16)
                send_ref[:, vcols] = dv[p * tok_rows : (p + 1) * tok_rows].astype(jnp.bfloat16)

    return pl.pallas_call(
        kernel,
        out_shape=(jax.ShapeDtypeStruct((tok_rows, 2 * kv_cols), jnp.float32),)
        + tuple(
            jax.ShapeDtypeStruct((tok_rows, 2 * kv_cols), jnp.bfloat16) for _ in range(n_blocks - 1)
        ),
    )(q3, g3, *kv_blocks, lower, upper)


def per_device(inputs, query, grad_out, w_key, w_value, keep_mask):
    tok_rows = inputs.shape[1]
    local_heads = query.shape[2]
    head_dim = query.shape[3]
    kv_cols = w_key.shape[2]
    kv_local = kv_cols // head_dim
    group_size = local_heads // kv_local
    scaling = 1.0 / math.sqrt(head_dim)
    ctx_len = lax.axis_size("ctx")
    ctx_index = lax.axis_index("ctx")
    tokens = inputs[0]
    key_rows = jnp.dot(tokens, w_key[0], preferred_element_type=jnp.float32).astype(jnp.bfloat16)
    value_rows = jnp.dot(tokens, w_value[0], preferred_element_type=jnp.float32).astype(
        jnp.bfloat16
    )
    kv_own = jnp.concatenate((key_rows, value_rows), axis=1)
    later = {d: shifted(kv_own, "ctx", d, ctx_len, True) for d in range(ctx_len - 1, 0, -1)}
    blocks = [kv_own] + [later[d] for d in range(1, ctx_len)]
    seq_rows = tok_rows * ctx_len
    first_row = ctx_index * tok_rows
    blk = jnp.arange(ctx_len, dtype=jnp.int32)
    col_pos = (
        (ctx_index - blk)[:, None] * tok_rows + jnp.arange(tok_rows, dtype=jnp.int32)[None, :]
    ).reshape(seq_rows, 1)
    keep_blocks = keep_mask.reshape(ctx_len, tok_rows)
    kept = jnp.concatenate(
        [
            lax.dynamic_index_in_dim(keep_blocks, jnp.maximum(ctx_index - p, 0), 0, keepdims=False)
            for p in range(ctx_len)
        ],
        axis=0,
    ).reshape(seq_rows, 1)
    never = jnp.iinfo(jnp.int32).max
    lower = jnp.where(col_pos >= 0, col_pos - first_row, never)
    upper = jnp.where(kept == 1, never, col_pos - first_row)
    q3 = jnp.transpose(query[0], (1, 0, 2))
    g3 = jnp.transpose(grad_out[0], (1, 0, 2))
    kv_grad, *parts = attention_terms(q3, g3, blocks, lower, upper, kv_local, head_dim, scaling)
    for d in range(1, ctx_len):
        part = parts[d - 1]
        kv_grad = kv_grad + shifted(part, "ctx", d, ctx_len, False).astype(jnp.float32)
    grad_key = kv_grad[:, :kv_cols].astype(jnp.bfloat16)
    grad_value = kv_grad[:, kv_cols:].astype(jnp.bfloat16)
    contract = (((1,), (1,)), ((), ()))
    head_len = lax.axis_size("head")
    head_index = lax.axis_index("head")
    out_cols = w_key.shape[1] // head_len

    def partial_for(b):
        start = b * out_cols
        wk = lax.dynamic_slice_in_dim(w_key[0], start, out_cols, axis=0)
        wv = lax.dynamic_slice_in_dim(w_value[0], start, out_cols, axis=0)
        part = lax.dot_general(grad_key, wk, contract, preferred_element_type=jnp.float32)
        return part + lax.dot_general(grad_value, wv, contract, preferred_element_type=jnp.float32)

    received = []
    for d in range(1, head_len):
        target = lax.rem(head_index + d, head_len)
        send = partial_for(target).astype(jnp.bfloat16)
        perm = [(h, (h + d) % head_len) for h in range(head_len)]
        received.append(lax.ppermute(send, "head", perm))
    reduced = partial_for(head_index)
    for got in received:
        reduced = reduced + got.astype(jnp.float32)
    result = suffix_pipeline(reduced, "segment", CHAIN_CHUNKS)
    return result[None]


def solution(mesh):
    return jax.shard_map(
        per_device,
        mesh=mesh,
        in_specs=(
            P("segment", "ctx", None),
            P("segment", "ctx", "head", None),
            P("segment", "ctx", "head", None),
            P("segment", None, "head"),
            P("segment", None, "head"),
            P(),
        ),
        out_specs=P("segment", "ctx", "head"),
        check_vma=False,
    )
```

```python
import math

import jax
import jax.numpy as jnp
from jax import lax
from jax.experimental import pallas as pl
from jax.sharding import PartitionSpec as P


CHAIN_CHUNKS = 2


def shifted(x, axis, d, length, up):
    if up:
        perm = [(c, c + d) for c in range(length - d)]
    else:
        perm = [(c, c - d) for c in range(d, length)]
    return lax.ppermute(x, axis, perm)


def suffix_pipeline(own, axis, n_chunks):
    length, index = (lax.axis_size(axis), lax.axis_index(axis))
    rows, cols = own.shape
    height = rows // n_chunks
    chunks = own.reshape(n_chunks, height, cols)
    pad = jnp.zeros((length - 1, height, cols), own.dtype)
    padded = jnp.concatenate((pad, chunks, pad), axis=0)
    steps = n_chunks + length - 1
    ordered = lax.dynamic_slice_in_dim(padded, index, steps, axis=0)
    perm = [(i, i - 1) for i in range(1, length)]
    recv = jnp.zeros((height, cols), jnp.bfloat16)
    done = []
    for tau in range(steps):
        acc = ordered[tau] + recv.astype(jnp.float32)
        done.append(acc)
        if tau < steps - 1:
            recv = lax.ppermute(acc.astype(jnp.bfloat16), axis, perm)
    stacked = jnp.stack(done, axis=0)
    mine = lax.dynamic_slice_in_dim(stacked, length - 1 - index, n_chunks, axis=0)
    return mine.reshape(rows, cols)


def attention_terms(q3, g3, kv_blocks, lower, upper, kv_local, head_dim, scaling):
    tok_rows = q3.shape[1]
    group = q3.shape[0] // kv_local
    n_blocks = len(kv_blocks)
    seq_rows = tok_rows * n_blocks
    kv_cols = kv_local * head_dim
    nt = (((1,), (1,)), ((), ()))

    def kernel(*refs):
        q_ref, g_ref = refs[0], refs[1]
        kv_refs = refs[2 : 2 + n_blocks]
        lo_ref, hi_ref, own_ref = refs[2 + n_blocks : 5 + n_blocks]
        send_refs = refs[5 + n_blocks :]
        rows = lax.broadcasted_iota(jnp.int32, (seq_rows, tok_rows), 1)
        allowed = (lo_ref[...] <= rows) & (rows <= hi_ref[...])
        for k in range(kv_local):
            kcols = slice(k * head_dim, (k + 1) * head_dim)
            vcols = slice(kv_cols + k * head_dim, kv_cols + (k + 1) * head_dim)
            key = jnp.concatenate([r[:, kcols] for r in kv_refs], axis=0)
            val = jnp.concatenate([r[:, vcols] for r in kv_refs], axis=0)
            dk = jnp.zeros((seq_rows, head_dim), jnp.float32)
            dv = jnp.zeros((seq_rows, head_dim), jnp.float32)
            for j in range(group):
                h = k * group + j
                q = q_ref[h]
                gr = g_ref[h]
                s = lax.dot_general(key, q, nt, preferred_element_type=jnp.float32) * scaling
                masked = jnp.where(allowed, s, -1e30)
                top = jnp.max(masked, axis=0, keepdims=True)
                e = jnp.where(allowed, jnp.exp(masked - top), 0.0)
                tot = jnp.sum(e, axis=0, keepdims=True)
                p = e * (1.0 / tot)
                pb = p.astype(jnp.bfloat16)
                dp = lax.dot_general(val, gr, nt, preferred_element_type=jnp.float32)
                rd = jnp.sum(pb.astype(jnp.float32) * dp, axis=0, keepdims=True)
                ds = (p * (dp - rd)).astype(jnp.bfloat16)
                dv = dv + jnp.dot(pb, gr, preferred_element_type=jnp.float32)
                dk = dk + jnp.dot(ds, q, preferred_element_type=jnp.float32)
            dk = dk * scaling
            own_ref[:, kcols] = dk[:tok_rows]
            own_ref[:, vcols] = dv[:tok_rows]
            for p, send_ref in enumerate(send_refs, start=1):
                send_ref[:, kcols] = dk[p * tok_rows : (p + 1) * tok_rows].astype(jnp.bfloat16)
                send_ref[:, vcols] = dv[p * tok_rows : (p + 1) * tok_rows].astype(jnp.bfloat16)

    return pl.pallas_call(
        kernel,
        out_shape=(jax.ShapeDtypeStruct((tok_rows, 2 * kv_cols), jnp.float32),)
        + tuple(
            jax.ShapeDtypeStruct((tok_rows, 2 * kv_cols), jnp.bfloat16) for _ in range(n_blocks - 1)
        ),
    )(q3, g3, *kv_blocks, lower, upper)


def per_device(inputs, query, grad_out, w_key, w_value, keep_mask):
    tok_rows = inputs.shape[1]
    local_heads = query.shape[2]
    head_dim = query.shape[3]
    kv_cols = w_key.shape[2]
    kv_local = kv_cols // head_dim
    group_size = local_heads // kv_local
    scaling = 1.0 / math.sqrt(head_dim)
    ctx_len = lax.axis_size("ctx")
    ctx_index = lax.axis_index("ctx")
    tokens = inputs[0]
    key_rows = jnp.dot(tokens, w_key[0], preferred_element_type=jnp.float32).astype(jnp.bfloat16)
    value_rows = jnp.dot(tokens, w_value[0], preferred_element_type=jnp.float32).astype(
        jnp.bfloat16
    )
    kv_own = jnp.concatenate((key_rows, value_rows), axis=1)
    later = {d: shifted(kv_own, "ctx", d, ctx_len, True) for d in range(ctx_len - 1, 0, -1)}
    blocks = [kv_own] + [later[d] for d in range(1, ctx_len)]
    seq_rows = tok_rows * ctx_len
    first_row = ctx_index * tok_rows
    blk = jnp.arange(ctx_len, dtype=jnp.int32)
    col_pos = (
        (ctx_index - blk)[:, None] * tok_rows + jnp.arange(tok_rows, dtype=jnp.int32)[None, :]
    ).reshape(seq_rows, 1)
    keep_blocks = keep_mask.reshape(ctx_len, tok_rows)
    kept = jnp.concatenate(
        [
            lax.dynamic_index_in_dim(keep_blocks, jnp.maximum(ctx_index - p, 0), 0, keepdims=False)
            for p in range(ctx_len)
        ],
        axis=0,
    ).reshape(seq_rows, 1)
    never = jnp.iinfo(jnp.int32).max
    lower = jnp.where(col_pos >= 0, col_pos - first_row, never)
    upper = jnp.where(kept == 1, never, col_pos - first_row)
    q3 = jnp.transpose(query[0], (1, 0, 2))
    g3 = jnp.transpose(grad_out[0], (1, 0, 2))
    kv_grad, *parts = attention_terms(q3, g3, blocks, lower, upper, kv_local, head_dim, scaling)
    for d in range(1, ctx_len):
        part = parts[d - 1]
        kv_grad = kv_grad + shifted(part, "ctx", d, ctx_len, False).astype(jnp.float32)
    grads_low = kv_grad.astype(jnp.bfloat16)
    contract = (((1,), (1,)), ((), ()))
    head_len = lax.axis_size("head")
    head_index = lax.axis_index("head")
    out_cols = w_key.shape[1] // head_len

    def rows_of(b):
        start = b * out_cols
        wk = lax.dynamic_slice_in_dim(w_key[0], start, out_cols, axis=0)
        wv = lax.dynamic_slice_in_dim(w_value[0], start, out_cols, axis=0)
        return wk, wv

    def product(grads, wk, wv):
        part = lax.dot_general(grads[:, :kv_cols], wk, contract, preferred_element_type=jnp.float32)
        return part + lax.dot_general(
            grads[:, kv_cols:], wv, contract, preferred_element_type=jnp.float32
        )

    sources = []
    for d in range(1, head_len):
        perm = [(h, (h + d) % head_len) for h in range(head_len)]
        wk, wv = rows_of(lax.rem(head_index + d, head_len))
        weights = lax.ppermute(jnp.concatenate((wk, wv), axis=1), "head", perm)
        sources.append((lax.ppermute(grads_low, "head", perm), weights))
    reduced = product(grads_low, *rows_of(head_index))
    for grads, weights in sources:
        reduced = reduced + product(grads, weights[:, :kv_cols], weights[:, kv_cols:])
    result = suffix_pipeline(reduced, "segment", CHAIN_CHUNKS)
    return result[None]


def solution(mesh):
    return jax.shard_map(
        per_device,
        mesh=mesh,
        in_specs=(
            P("segment", "ctx", None),
            P("segment", "ctx", "head", None),
            P("segment", "ctx", "head", None),
            P("segment", None, "head"),
            P("segment", None, "head"),
            P(),
        ),
        out_specs=P("segment", "ctx", "head"),
        check_vma=False,
    )
```

```python
import math

import jax
import jax.numpy as jnp
from jax import lax
from jax.experimental import pallas as pl
from jax.experimental.pallas import tpu as pltpu
from jax.sharding import PartitionSpec as P


CHAIN_CHUNKS = 2


def shifted(x, axis, d, length, up):
    if up:
        perm = [(c, c + d) for c in range(length - d)]
    else:
        perm = [(c, c - d) for c in range(d, length)]
    return lax.ppermute(x, axis, perm)


def suffix_pipeline(own, axis, n_chunks):
    length, index = (lax.axis_size(axis), lax.axis_index(axis))
    rows, cols = own.shape
    height = rows // n_chunks
    chunks = own.reshape(n_chunks, height, cols)
    pad = jnp.zeros((length - 1, height, cols), own.dtype)
    padded = jnp.concatenate((pad, chunks, pad), axis=0)
    steps = n_chunks + length - 1
    ordered = lax.dynamic_slice_in_dim(padded, index, steps, axis=0)
    perm = [(i, i - 1) for i in range(1, length)]
    recv = jnp.zeros((height, cols), jnp.bfloat16)
    done = []
    for tau in range(steps):
        acc = ordered[tau] + recv.astype(jnp.float32)
        done.append(acc)
        if tau < steps - 1:
            recv = lax.ppermute(acc.astype(jnp.bfloat16), axis, perm)
    stacked = jnp.stack(done, axis=0)
    mine = lax.dynamic_slice_in_dim(stacked, length - 1 - index, n_chunks, axis=0)
    return mine.reshape(rows, cols)


def attention_terms(q3, g3, kv_blocks, lower, upper, kv_local, head_dim, scaling):
    tok_rows = q3.shape[1]
    group = q3.shape[0] // kv_local
    n_blocks = len(kv_blocks)
    seq_rows = tok_rows * n_blocks
    kv_cols = kv_local * head_dim
    nt = (((1,), (1,)), ((), ()))

    def kernel(*refs):
        q_ref, g_ref = refs[0], refs[1]
        kv_refs = refs[2 : 2 + n_blocks]
        lo_ref, hi_ref, own_ref = refs[2 + n_blocks : 5 + n_blocks]
        send_refs = refs[5 + n_blocks :]
        rows = lax.broadcasted_iota(jnp.int32, (seq_rows, tok_rows), 1)
        allowed = (lo_ref[...] <= rows) & (rows <= hi_ref[...])
        for k in range(kv_local):
            kcols = slice(k * head_dim, (k + 1) * head_dim)
            vcols = slice(kv_cols + k * head_dim, kv_cols + (k + 1) * head_dim)
            key = jnp.concatenate([r[:, kcols] for r in kv_refs], axis=0)
            val = jnp.concatenate([r[:, vcols] for r in kv_refs], axis=0)
            dk = jnp.zeros((seq_rows, head_dim), jnp.float32)
            dv = jnp.zeros((seq_rows, head_dim), jnp.float32)
            for j in range(group):
                h = k * group + j
                q = q_ref[h]
                gr = g_ref[h]
                s = lax.dot_general(key, q, nt, preferred_element_type=jnp.float32) * scaling
                masked = jnp.where(allowed, s, -1e30)
                top = jnp.max(masked, axis=0, keepdims=True)
                e = jnp.where(allowed, jnp.exp(masked - top), 0.0)
                tot = jnp.sum(e, axis=0, keepdims=True)
                p = e * (1.0 / tot)
                pb = p.astype(jnp.bfloat16)
                dp = lax.dot_general(val, gr, nt, preferred_element_type=jnp.float32)
                rd = jnp.sum(pb.astype(jnp.float32) * dp, axis=0, keepdims=True)
                ds = (p * (dp - rd)).astype(jnp.bfloat16)
                dv = dv + jnp.dot(pb, gr, preferred_element_type=jnp.float32)
                dk = dk + jnp.dot(ds, q, preferred_element_type=jnp.float32)
            dk = dk * scaling
            own_ref[:, kcols] = dk[:tok_rows]
            own_ref[:, vcols] = dv[:tok_rows]
            for p, send_ref in enumerate(send_refs, start=1):
                send_ref[:, kcols] = dk[p * tok_rows : (p + 1) * tok_rows].astype(jnp.bfloat16)
                send_ref[:, vcols] = dv[p * tok_rows : (p + 1) * tok_rows].astype(jnp.bfloat16)

    return pl.pallas_call(
        kernel,
        out_shape=(jax.ShapeDtypeStruct((tok_rows, 2 * kv_cols), jnp.float32),)
        + tuple(
            jax.ShapeDtypeStruct((tok_rows, 2 * kv_cols), jnp.bfloat16) for _ in range(n_blocks - 1)
        ),
    )(q3, g3, *kv_blocks, lower, upper)


def projections(tokens, wk, wv, depth):
    rows, width = tokens.shape
    cols = wk.shape[1]
    steps = width // depth

    def kernel(t_ref, k_ref, v_ref, out_ref, acc_ref):
        step = pl.program_id(0)

        @pl.when(step == 0)
        def _():
            acc_ref[...] = jnp.zeros_like(acc_ref)

        t = t_ref[...]
        acc_ref[:, :cols] += jnp.dot(t, k_ref[...], preferred_element_type=jnp.float32)
        acc_ref[:, cols:] += jnp.dot(t, v_ref[...], preferred_element_type=jnp.float32)

        @pl.when(step == steps - 1)
        def _():
            out_ref[...] = acc_ref[...].astype(out_ref.dtype)

    return pl.pallas_call(
        kernel,
        grid=(steps,),
        in_specs=[
            pl.BlockSpec((rows, depth), lambda i: (0, i)),
            pl.BlockSpec((depth, cols), lambda i: (i, 0)),
            pl.BlockSpec((depth, cols), lambda i: (i, 0)),
        ],
        out_specs=pl.BlockSpec((rows, 2 * cols), lambda i: (0, 0)),
        out_shape=jax.ShapeDtypeStruct((rows, 2 * cols), jnp.bfloat16),
        scratch_shapes=[pltpu.VMEM((rows, 2 * cols), jnp.float32)],
    )(tokens, wk, wv)


def per_device(inputs, query, grad_out, w_key, w_value, keep_mask):
    tok_rows = inputs.shape[1]
    local_heads = query.shape[2]
    head_dim = query.shape[3]
    kv_cols = w_key.shape[2]
    kv_local = kv_cols // head_dim
    group_size = local_heads // kv_local
    scaling = 1.0 / math.sqrt(head_dim)
    ctx_len = lax.axis_size("ctx")
    ctx_index = lax.axis_index("ctx")
    tokens = inputs[0]
    kv_own = projections(tokens, w_key[0], w_value[0], 1024)
    later = {d: shifted(kv_own, "ctx", d, ctx_len, True) for d in range(ctx_len - 1, 0, -1)}
    blocks = [kv_own] + [later[d] for d in range(1, ctx_len)]
    seq_rows = tok_rows * ctx_len
    first_row = ctx_index * tok_rows
    blk = jnp.arange(ctx_len, dtype=jnp.int32)
    col_pos = (
        (ctx_index - blk)[:, None] * tok_rows + jnp.arange(tok_rows, dtype=jnp.int32)[None, :]
    ).reshape(seq_rows, 1)
    keep_blocks = keep_mask.reshape(ctx_len, tok_rows)
    kept = jnp.concatenate(
        [
            lax.dynamic_index_in_dim(keep_blocks, jnp.maximum(ctx_index - p, 0), 0, keepdims=False)
            for p in range(ctx_len)
        ],
        axis=0,
    ).reshape(seq_rows, 1)
    never = jnp.iinfo(jnp.int32).max
    lower = jnp.where(col_pos >= 0, col_pos - first_row, never)
    upper = jnp.where(kept == 1, never, col_pos - first_row)
    q3 = jnp.transpose(query[0], (1, 0, 2))
    g3 = jnp.transpose(grad_out[0], (1, 0, 2))
    kv_grad, *parts = attention_terms(q3, g3, blocks, lower, upper, kv_local, head_dim, scaling)
    for d in range(1, ctx_len):
        part = parts[d - 1]
        kv_grad = kv_grad + shifted(part, "ctx", d, ctx_len, False).astype(jnp.float32)
    grad_key = kv_grad[:, :kv_cols].astype(jnp.bfloat16)
    grad_value = kv_grad[:, kv_cols:].astype(jnp.bfloat16)
    contract = (((1,), (1,)), ((), ()))
    head_len = lax.axis_size("head")
    head_index = lax.axis_index("head")
    out_cols = w_key.shape[1] // head_len

    def partial_for(b):
        start = b * out_cols
        wk = lax.dynamic_slice_in_dim(w_key[0], start, out_cols, axis=0)
        wv = lax.dynamic_slice_in_dim(w_value[0], start, out_cols, axis=0)
        part = lax.dot_general(grad_key, wk, contract, preferred_element_type=jnp.float32)
        return part + lax.dot_general(grad_value, wv, contract, preferred_element_type=jnp.float32)

    received = []
    for d in range(1, head_len):
        target = lax.rem(head_index + d, head_len)
        send = partial_for(target).astype(jnp.bfloat16)
        perm = [(h, (h + d) % head_len) for h in range(head_len)]
        received.append(lax.ppermute(send, "head", perm))
    reduced = partial_for(head_index)
    for got in received:
        reduced = reduced + got.astype(jnp.float32)
    result = suffix_pipeline(reduced, "segment", CHAIN_CHUNKS)
    return result[None]


def solution(mesh):
    return jax.shard_map(
        per_device,
        mesh=mesh,
        in_specs=(
            P("segment", "ctx", None),
            P("segment", "ctx", "head", None),
            P("segment", "ctx", "head", None),
            P("segment", None, "head"),
            P("segment", None, "head"),
            P(),
        ),
        out_specs=P("segment", "ctx", "head"),
        check_vma=False,
    )
```

```python
import math

import jax
import jax.numpy as jnp
from jax import lax
from jax.experimental import pallas as pl
from jax.sharding import PartitionSpec as P


CHAIN_CHUNKS = 2


def shifted(x, axis, d, length, up):
    if up:
        perm = [(c, c + d) for c in range(length - d)]
    else:
        perm = [(c, c - d) for c in range(d, length)]
    return lax.ppermute(x, axis, perm)


def suffix_pipeline(pieces, axis):
    length, index = (lax.axis_size(axis), lax.axis_index(axis))
    n_chunks = len(pieces)
    height, cols = pieces[0].shape
    rows = n_chunks * height
    own = pieces[0].dtype
    chunks = jnp.stack(pieces, axis=0)
    pad = jnp.zeros((length - 1, height, cols), own)
    padded = jnp.concatenate((pad, chunks, pad), axis=0)
    steps = n_chunks + length - 1
    ordered = lax.dynamic_slice_in_dim(padded, index, steps, axis=0)
    perm = [(i, i - 1) for i in range(1, length)]
    recv = jnp.zeros((height, cols), jnp.bfloat16)
    done = []
    for tau in range(steps):
        acc = (pieces[0] if tau == 0 else ordered[tau]) + recv.astype(jnp.float32)
        done.append(acc)
        if tau < steps - 1:
            recv = lax.ppermute(acc.astype(jnp.bfloat16), axis, perm)
    stacked = jnp.stack(done, axis=0)
    mine = lax.dynamic_slice_in_dim(stacked, length - 1 - index, n_chunks, axis=0)
    return mine.reshape(rows, cols)


def attention_terms(q3, g3, kv_blocks, lower, upper, kv_local, head_dim, scaling):
    tok_rows = q3.shape[1]
    group = q3.shape[0] // kv_local
    n_blocks = len(kv_blocks)
    seq_rows = tok_rows * n_blocks
    kv_cols = kv_local * head_dim
    nt = (((1,), (1,)), ((), ()))

    def kernel(*refs):
        q_ref, g_ref = refs[0], refs[1]
        kv_refs = refs[2 : 2 + n_blocks]
        lo_ref, hi_ref, own_ref = refs[2 + n_blocks : 5 + n_blocks]
        send_refs = refs[5 + n_blocks :]
        rows = lax.broadcasted_iota(jnp.int32, (seq_rows, tok_rows), 1)
        allowed = (lo_ref[...] <= rows) & (rows <= hi_ref[...])
        for k in range(kv_local):
            kcols = slice(k * head_dim, (k + 1) * head_dim)
            vcols = slice(kv_cols + k * head_dim, kv_cols + (k + 1) * head_dim)
            key = jnp.concatenate([r[:, kcols] for r in kv_refs], axis=0)
            val = jnp.concatenate([r[:, vcols] for r in kv_refs], axis=0)
            dk = jnp.zeros((seq_rows, head_dim), jnp.float32)
            dv = jnp.zeros((seq_rows, head_dim), jnp.float32)
            for j in range(group):
                h = k * group + j
                q = q_ref[h]
                gr = g_ref[h]
                s = lax.dot_general(key, q, nt, preferred_element_type=jnp.float32) * scaling
                masked = jnp.where(allowed, s, -1e30)
                top = jnp.max(masked, axis=0, keepdims=True)
                e = jnp.where(allowed, jnp.exp(masked - top), 0.0)
                tot = jnp.sum(e, axis=0, keepdims=True)
                p = e * (1.0 / tot)
                pb = p.astype(jnp.bfloat16)
                dp = lax.dot_general(val, gr, nt, preferred_element_type=jnp.float32)
                rd = jnp.sum(pb.astype(jnp.float32) * dp, axis=0, keepdims=True)
                ds = (p * (dp - rd)).astype(jnp.bfloat16)
                dv = dv + jnp.dot(pb, gr, preferred_element_type=jnp.float32)
                dk = dk + jnp.dot(ds, q, preferred_element_type=jnp.float32)
            dk = dk * scaling
            own_ref[:, kcols] = dk[:tok_rows]
            own_ref[:, vcols] = dv[:tok_rows]
            for p, send_ref in enumerate(send_refs, start=1):
                send_ref[:, kcols] = dk[p * tok_rows : (p + 1) * tok_rows].astype(jnp.bfloat16)
                send_ref[:, vcols] = dv[p * tok_rows : (p + 1) * tok_rows].astype(jnp.bfloat16)

    return pl.pallas_call(
        kernel,
        out_shape=(jax.ShapeDtypeStruct((tok_rows, 2 * kv_cols), jnp.float32),)
        + tuple(
            jax.ShapeDtypeStruct((tok_rows, 2 * kv_cols), jnp.bfloat16) for _ in range(n_blocks - 1)
        ),
    )(q3, g3, *kv_blocks, lower, upper)


def per_device(inputs, query, grad_out, w_key, w_value, keep_mask):
    tok_rows = inputs.shape[1]
    local_heads = query.shape[2]
    head_dim = query.shape[3]
    kv_cols = w_key.shape[2]
    kv_local = kv_cols // head_dim
    group_size = local_heads // kv_local
    scaling = 1.0 / math.sqrt(head_dim)
    ctx_len = lax.axis_size("ctx")
    ctx_index = lax.axis_index("ctx")
    tokens = inputs[0]
    key_rows = jnp.dot(tokens, w_key[0], preferred_element_type=jnp.float32).astype(jnp.bfloat16)
    value_rows = jnp.dot(tokens, w_value[0], preferred_element_type=jnp.float32).astype(
        jnp.bfloat16
    )
    kv_own = jnp.concatenate((key_rows, value_rows), axis=1)
    later = {d: shifted(kv_own, "ctx", d, ctx_len, True) for d in range(ctx_len - 1, 0, -1)}
    blocks = [kv_own] + [later[d] for d in range(1, ctx_len)]
    seq_rows = tok_rows * ctx_len
    first_row = ctx_index * tok_rows
    blk = jnp.arange(ctx_len, dtype=jnp.int32)
    col_pos = (
        (ctx_index - blk)[:, None] * tok_rows + jnp.arange(tok_rows, dtype=jnp.int32)[None, :]
    ).reshape(seq_rows, 1)
    keep_blocks = keep_mask.reshape(ctx_len, tok_rows)
    kept = jnp.concatenate(
        [
            lax.dynamic_index_in_dim(keep_blocks, jnp.maximum(ctx_index - p, 0), 0, keepdims=False)
            for p in range(ctx_len)
        ],
        axis=0,
    ).reshape(seq_rows, 1)
    never = jnp.iinfo(jnp.int32).max
    lower = jnp.where(col_pos >= 0, col_pos - first_row, never)
    upper = jnp.where(kept == 1, never, col_pos - first_row)
    q3 = jnp.transpose(query[0], (1, 0, 2))
    g3 = jnp.transpose(grad_out[0], (1, 0, 2))
    kv_grad, *parts = attention_terms(q3, g3, blocks, lower, upper, kv_local, head_dim, scaling)
    for d in range(1, ctx_len):
        part = parts[d - 1]
        kv_grad = kv_grad + shifted(part, "ctx", d, ctx_len, False).astype(jnp.float32)
    grad_key = kv_grad[:, :kv_cols].astype(jnp.bfloat16)
    grad_value = kv_grad[:, kv_cols:].astype(jnp.bfloat16)
    contract = (((1,), (1,)), ((), ()))
    head_len = lax.axis_size("head")
    head_index = lax.axis_index("head")
    out_cols = w_key.shape[1] // head_len

    height = tok_rows // CHAIN_CHUNKS

    def partial_for(b, rows):
        start = b * out_cols
        wk = lax.dynamic_slice_in_dim(w_key[0], start, out_cols, axis=0)
        wv = lax.dynamic_slice_in_dim(w_value[0], start, out_cols, axis=0)
        part = lax.dot_general(grad_key[rows], wk, contract, preferred_element_type=jnp.float32)
        return part + lax.dot_general(
            grad_value[rows], wv, contract, preferred_element_type=jnp.float32
        )

    pieces = []
    for c in range(CHAIN_CHUNKS):
        rows = slice(c * height, (c + 1) * height)
        received = []
        for d in range(1, head_len):
            target = lax.rem(head_index + d, head_len)
            send = partial_for(target, rows).astype(jnp.bfloat16)
            perm = [(h, (h + d) % head_len) for h in range(head_len)]
            received.append(lax.ppermute(send, "head", perm))
        reduced = partial_for(head_index, rows)
        for got in received:
            reduced = reduced + got.astype(jnp.float32)
        pieces.append(reduced)
    result = suffix_pipeline(pieces, "segment")
    return result[None]


def solution(mesh):
    return jax.shard_map(
        per_device,
        mesh=mesh,
        in_specs=(
            P("segment", "ctx", None),
            P("segment", "ctx", "head", None),
            P("segment", "ctx", "head", None),
            P("segment", None, "head"),
            P("segment", None, "head"),
            P(),
        ),
        out_specs=P("segment", "ctx", "head"),
        check_vma=False,
    )
```

```python
import math

import jax
import jax.numpy as jnp
from jax import lax
from jax.experimental import pallas as pl
from jax.sharding import PartitionSpec as P


CHAIN_CHUNKS = 2


def shifted(x, axis, d, length, up):
    if up:
        perm = [(c, c + d) for c in range(length - d)]
    else:
        perm = [(c, c - d) for c in range(d, length)]
    return lax.ppermute(x, axis, perm)


def suffix_pipeline(own, axis, n_chunks):
    length, index = (lax.axis_size(axis), lax.axis_index(axis))
    rows, cols = own.shape
    height = rows // n_chunks
    chunks = own.reshape(n_chunks, height, cols)
    pad = jnp.zeros((length - 1, height, cols), own.dtype)
    padded = jnp.concatenate((pad, chunks, pad), axis=0)
    steps = n_chunks + length - 1
    ordered = lax.dynamic_slice_in_dim(padded, index, steps, axis=0)
    perm = [(i, i - 1) for i in range(1, length)]
    recv = jnp.zeros((height, cols), jnp.bfloat16)
    done = []
    for tau in range(steps):
        acc = (chunks[0] if tau == 0 else ordered[tau]) + recv.astype(jnp.float32)
        done.append(acc)
        if tau < steps - 1:
            recv = lax.ppermute(acc.astype(jnp.bfloat16), axis, perm)
    stacked = jnp.stack(done, axis=0)
    mine = lax.dynamic_slice_in_dim(stacked, length - 1 - index, n_chunks, axis=0)
    return mine.reshape(rows, cols)


def attention_terms(q3, g3, kv_blocks, lower, upper, kv_local, head_dim, scaling):
    tok_rows = q3.shape[1]
    group = q3.shape[0] // kv_local
    n_blocks = len(kv_blocks)
    seq_rows = tok_rows * n_blocks
    kv_cols = kv_local * head_dim
    nt = (((1,), (1,)), ((), ()))

    def kernel(*refs):
        q_ref, g_ref = refs[0], refs[1]
        kv_refs = refs[2 : 2 + n_blocks]
        lo_ref, hi_ref, own_ref = refs[2 + n_blocks : 5 + n_blocks]
        send_refs = refs[5 + n_blocks :]
        rows = lax.broadcasted_iota(jnp.int32, (seq_rows, tok_rows), 1)
        allowed = (lo_ref[...] <= rows) & (rows <= hi_ref[...])
        for k in range(kv_local):
            kcols = slice(k * head_dim, (k + 1) * head_dim)
            vcols = slice(kv_cols + k * head_dim, kv_cols + (k + 1) * head_dim)
            key = jnp.concatenate([r[:, kcols] for r in kv_refs], axis=0)
            val = jnp.concatenate([r[:, vcols] for r in kv_refs], axis=0)
            dk = jnp.zeros((seq_rows, head_dim), jnp.float32)
            dv = jnp.zeros((seq_rows, head_dim), jnp.float32)
            for j in range(group):
                h = k * group + j
                q = q_ref[h]
                gr = g_ref[h]
                s = lax.dot_general(key, q, nt, preferred_element_type=jnp.float32) * scaling
                masked = jnp.where(allowed, s, -1e30)
                top = jnp.max(masked, axis=0, keepdims=True)
                e = jnp.where(allowed, jnp.exp(masked - top), 0.0)
                tot = jnp.sum(e, axis=0, keepdims=True)
                p = e * (1.0 / tot)
                pb = p.astype(jnp.bfloat16)
                dp = lax.dot_general(val, gr, nt, preferred_element_type=jnp.float32)
                rd = jnp.sum(pb.astype(jnp.float32) * dp, axis=0, keepdims=True)
                ds = (p * (dp - rd)).astype(jnp.bfloat16)
                dv = dv + jnp.dot(pb, gr, preferred_element_type=jnp.float32)
                dk = dk + jnp.dot(ds, q, preferred_element_type=jnp.float32)
            dk = dk * scaling
            own_ref[:, kcols] = dk[:tok_rows]
            own_ref[:, vcols] = dv[:tok_rows]
            for p, send_ref in enumerate(send_refs, start=1):
                send_ref[:, kcols] = dk[p * tok_rows : (p + 1) * tok_rows].astype(jnp.bfloat16)
                send_ref[:, vcols] = dv[p * tok_rows : (p + 1) * tok_rows].astype(jnp.bfloat16)

    return pl.pallas_call(
        kernel,
        out_shape=(jax.ShapeDtypeStruct((tok_rows, 2 * kv_cols), jnp.float32),)
        + tuple(
            jax.ShapeDtypeStruct((tok_rows, 2 * kv_cols), jnp.bfloat16) for _ in range(n_blocks - 1)
        ),
    )(q3, g3, *kv_blocks, lower, upper)


def per_device(inputs, query, grad_out, w_key, w_value, keep_mask):
    tok_rows = inputs.shape[1]
    local_heads = query.shape[2]
    head_dim = query.shape[3]
    kv_cols = w_key.shape[2]
    kv_local = kv_cols // head_dim
    group_size = local_heads // kv_local
    scaling = 1.0 / math.sqrt(head_dim)
    ctx_len = lax.axis_size("ctx")
    ctx_index = lax.axis_index("ctx")
    tokens = inputs[0]
    key_rows = jnp.dot(tokens, w_key[0], preferred_element_type=jnp.float32).astype(jnp.bfloat16)
    value_rows = jnp.dot(tokens, w_value[0], preferred_element_type=jnp.float32).astype(
        jnp.bfloat16
    )
    kv_own = jnp.concatenate((key_rows, value_rows), axis=1)
    later = {d: shifted(kv_own, "ctx", d, ctx_len, True) for d in range(ctx_len - 1, 0, -1)}
    blocks = [kv_own] + [later[d] for d in range(1, ctx_len)]
    seq_rows = tok_rows * ctx_len
    first_row = ctx_index * tok_rows
    blk = jnp.arange(ctx_len, dtype=jnp.int32)
    col_pos = (
        (ctx_index - blk)[:, None] * tok_rows + jnp.arange(tok_rows, dtype=jnp.int32)[None, :]
    ).reshape(seq_rows, 1)
    keep_blocks = keep_mask.reshape(ctx_len, tok_rows)
    kept = jnp.concatenate(
        [
            lax.dynamic_index_in_dim(keep_blocks, jnp.maximum(ctx_index - p, 0), 0, keepdims=False)
            for p in range(ctx_len)
        ],
        axis=0,
    ).reshape(seq_rows, 1)
    never = jnp.iinfo(jnp.int32).max
    lower = jnp.where(col_pos >= 0, col_pos - first_row, never)
    upper = jnp.where(kept == 1, never, col_pos - first_row)
    q3 = jnp.transpose(query[0], (1, 0, 2))
    g3 = jnp.transpose(grad_out[0], (1, 0, 2))
    kv_grad, *parts = attention_terms(q3, g3, blocks, lower, upper, kv_local, head_dim, scaling)
    for d in range(1, ctx_len):
        part = parts[d - 1]
        kv_grad = kv_grad + shifted(part, "ctx", d, ctx_len, False).astype(jnp.float32)
    grad_key = kv_grad[:, :kv_cols].astype(jnp.bfloat16)
    grad_value = kv_grad[:, kv_cols:].astype(jnp.bfloat16)
    contract = (((1,), (1,)), ((), ()))
    head_len = lax.axis_size("head")
    head_index = lax.axis_index("head")
    out_cols = w_key.shape[1] // head_len

    def partial_for(b):
        start = b * out_cols
        wk = lax.dynamic_slice_in_dim(w_key[0], start, out_cols, axis=0)
        wv = lax.dynamic_slice_in_dim(w_value[0], start, out_cols, axis=0)
        part = lax.dot_general(grad_key, wk, contract, preferred_element_type=jnp.float32)
        return part + lax.dot_general(grad_value, wv, contract, preferred_element_type=jnp.float32)

    received = []
    for d in range(1, head_len):
        target = lax.rem(head_index + d, head_len)
        send = partial_for(target).astype(jnp.bfloat16)
        perm = [(h, (h + d) % head_len) for h in range(head_len)]
        received.append(lax.ppermute(send, "head", perm))
    reduced = partial_for(head_index)
    for got in received:
        reduced = reduced + got.astype(jnp.float32)
    result = suffix_pipeline(reduced, "segment", CHAIN_CHUNKS)
    return result[None]


def solution(mesh):
    return jax.shard_map(
        per_device,
        mesh=mesh,
        in_specs=(
            P("segment", "ctx", None),
            P("segment", "ctx", "head", None),
            P("segment", "ctx", "head", None),
            P("segment", None, "head"),
            P("segment", None, "head"),
            P(),
        ),
        out_specs=P("segment", "ctx", "head"),
        check_vma=False,
    )
```

```python
import math

import jax
import jax.numpy as jnp
from jax import lax
from jax.experimental import pallas as pl
from jax.sharding import PartitionSpec as P


CHAIN_CHUNKS = 2


def shifted(x, axis, d, length, up):
    if up:
        perm = [(c, c + d) for c in range(length - d)]
    else:
        perm = [(c, c - d) for c in range(d, length)]
    return lax.ppermute(x, axis, perm)


def suffix_pipeline(own, axis, n_chunks):
    length, index = (lax.axis_size(axis), lax.axis_index(axis))
    rows, cols = own.shape
    height = rows // n_chunks
    chunks = own.reshape(n_chunks, height, cols)
    pad = jnp.zeros((length - 1, height, cols), own.dtype)
    padded = jnp.concatenate((pad, chunks, pad), axis=0)
    steps = n_chunks + length - 1
    ordered = lax.dynamic_slice_in_dim(padded, index, steps, axis=0)
    perm = [(i, i - 1) for i in range(1, length)]
    recv = jnp.zeros((height, cols), jnp.bfloat16)
    done = []
    for tau in range(steps):
        acc = (chunks[0] if tau == 0 else ordered[tau]) + recv.astype(jnp.float32)
        done.append(acc)
        if tau < steps - 1:
            recv = lax.ppermute(acc.astype(jnp.bfloat16), axis, perm)
    stacked = jnp.stack(done, axis=0)
    mine = lax.dynamic_slice_in_dim(stacked, length - 1 - index, n_chunks, axis=0)
    return mine.reshape(rows, cols)


def attention_terms(q3, g3, kv_blocks, lower, upper, kv_local, head_dim, scaling):
    tok_rows = q3.shape[1]
    group = q3.shape[0] // kv_local
    n_blocks = len(kv_blocks)
    seq_rows = tok_rows * n_blocks
    kv_cols = kv_local * head_dim
    nt = (((1,), (1,)), ((), ()))

    def kernel(*refs):
        q_ref, g_ref = refs[0], refs[1]
        kv_refs = refs[2 : 2 + n_blocks]
        lo_ref, hi_ref, own_ref = refs[2 + n_blocks : 5 + n_blocks]
        send_refs = refs[5 + n_blocks :]
        rows = lax.broadcasted_iota(jnp.int32, (seq_rows, tok_rows), 1)
        allowed = (lo_ref[...] <= rows) & (rows <= hi_ref[...])
        for k in range(kv_local):
            kcols = slice(k * head_dim, (k + 1) * head_dim)
            vcols = slice(kv_cols + k * head_dim, kv_cols + (k + 1) * head_dim)
            key = jnp.concatenate([r[:, kcols] for r in kv_refs], axis=0)
            val = jnp.concatenate([r[:, vcols] for r in kv_refs], axis=0)
            dk = jnp.zeros((seq_rows, head_dim), jnp.float32)
            dv = jnp.zeros((seq_rows, head_dim), jnp.float32)
            for j in range(group):
                h = k * group + j
                q = q_ref[h]
                gr = g_ref[h]
                s = lax.dot_general(key, q, nt, preferred_element_type=jnp.float32) * scaling
                masked = jnp.where(allowed, s, -1e30)
                top = jnp.max(masked, axis=0, keepdims=True)
                e = jnp.where(allowed, jnp.exp(masked - top), 0.0)
                tot = jnp.sum(e, axis=0, keepdims=True)
                p = e * (1.0 / tot)
                pb = p.astype(jnp.bfloat16)
                dp = lax.dot_general(val, gr, nt, preferred_element_type=jnp.float32)
                rd = jnp.sum(pb.astype(jnp.float32) * dp, axis=0, keepdims=True)
                ds = (p * (dp - rd)).astype(jnp.bfloat16)
                dv = dv + jnp.dot(pb, gr, preferred_element_type=jnp.float32)
                dk = dk + jnp.dot(ds, q, preferred_element_type=jnp.float32)
            dk = dk * scaling
            own_ref[:, kcols] = dk[:tok_rows]
            own_ref[:, vcols] = dv[:tok_rows]
            for p, send_ref in enumerate(send_refs, start=1):
                send_ref[:, kcols] = dk[p * tok_rows : (p + 1) * tok_rows].astype(jnp.bfloat16)
                send_ref[:, vcols] = dv[p * tok_rows : (p + 1) * tok_rows].astype(jnp.bfloat16)

    return pl.pallas_call(
        kernel,
        out_shape=(jax.ShapeDtypeStruct((tok_rows, 2 * kv_cols), jnp.float32),)
        + tuple(
            jax.ShapeDtypeStruct((tok_rows, 2 * kv_cols), jnp.bfloat16) for _ in range(n_blocks - 1)
        ),
    )(q3, g3, *kv_blocks, lower, upper)


def per_device(inputs, query, grad_out, w_key, w_value, keep_mask):
    tok_rows = inputs.shape[1]
    local_heads = query.shape[2]
    head_dim = query.shape[3]
    kv_cols = w_key.shape[2]
    kv_local = kv_cols // head_dim
    group_size = local_heads // kv_local
    scaling = 1.0 / math.sqrt(head_dim)
    ctx_len = lax.axis_size("ctx")
    ctx_index = lax.axis_index("ctx")
    tokens = inputs[0]
    key_rows = jnp.dot(tokens, w_key[0], preferred_element_type=jnp.float32).astype(jnp.bfloat16)
    value_rows = jnp.dot(tokens, w_value[0], preferred_element_type=jnp.float32).astype(
        jnp.bfloat16
    )
    kv_own = jnp.concatenate((key_rows, value_rows), axis=1)
    later = {d: shifted(kv_own, "ctx", d, ctx_len, True) for d in range(ctx_len - 1, 0, -1)}
    blocks = [kv_own] + [later[d] for d in range(1, ctx_len)]
    seq_rows = tok_rows * ctx_len
    first_row = ctx_index * tok_rows
    blk = jnp.arange(ctx_len, dtype=jnp.int32)
    col_pos = (
        (ctx_index - blk)[:, None] * tok_rows + jnp.arange(tok_rows, dtype=jnp.int32)[None, :]
    ).reshape(seq_rows, 1)
    keep_blocks = keep_mask.reshape(ctx_len, tok_rows)
    kept = jnp.concatenate(
        [
            lax.dynamic_index_in_dim(keep_blocks, jnp.maximum(ctx_index - p, 0), 0, keepdims=False)
            for p in range(ctx_len)
        ],
        axis=0,
    ).reshape(seq_rows, 1)
    never = jnp.iinfo(jnp.int32).max
    lower = jnp.where(col_pos >= 0, col_pos - first_row, never)
    upper = jnp.where(kept == 1, never, col_pos - first_row)
    q3 = jnp.transpose(query[0], (1, 0, 2))
    g3 = jnp.transpose(grad_out[0], (1, 0, 2))
    kv_grad, *parts = attention_terms(q3, g3, blocks, lower, upper, kv_local, head_dim, scaling)
    for d in range(1, ctx_len):
        part = parts[d - 1]
        kv_grad = kv_grad + shifted(part, "ctx", d, ctx_len, False).astype(jnp.float32)
    grad_key = kv_grad[:, :kv_cols].astype(jnp.bfloat16)
    grad_value = kv_grad[:, kv_cols:].astype(jnp.bfloat16)
    contract = (((1,), (1,)), ((), ()))
    head_len = lax.axis_size("head")
    head_index = lax.axis_index("head")
    out_cols = w_key.shape[1] // head_len

    def partial_for(b, width=out_cols, offset=0):
        start = b * out_cols + offset
        wk = lax.dynamic_slice_in_dim(w_key[0], start, width, axis=0)
        wv = lax.dynamic_slice_in_dim(w_value[0], start, width, axis=0)
        part = lax.dot_general(grad_key, wk, contract, preferred_element_type=jnp.float32)
        return part + lax.dot_general(grad_value, wv, contract, preferred_element_type=jnp.float32)

    half = out_cols // 2
    received = []
    for d in range(1, head_len):
        target = lax.rem(head_index + d, head_len)
        perm = [(h, (h + d) % head_len) for h in range(head_len)]
        pieces = [
            lax.ppermute(partial_for(target, half, i * half).astype(jnp.bfloat16), "head", perm)
            for i in range(2)
        ]
        received.append(jnp.concatenate(pieces, axis=1))
    reduced = partial_for(head_index)
    for got in received:
        reduced = reduced + got.astype(jnp.float32)
    result = suffix_pipeline(reduced, "segment", CHAIN_CHUNKS)
    return result[None]


def solution(mesh):
    return jax.shard_map(
        per_device,
        mesh=mesh,
        in_specs=(
            P("segment", "ctx", None),
            P("segment", "ctx", "head", None),
            P("segment", "ctx", "head", None),
            P("segment", None, "head"),
            P("segment", None, "head"),
            P(),
        ),
        out_specs=P("segment", "ctx", "head"),
        check_vma=False,
    )
```

```python
import math

import jax
import jax.numpy as jnp
from jax import lax
from jax.experimental import pallas as pl
from jax.sharding import PartitionSpec as P


CHAIN_CHUNKS = 2


def shifted(x, axis, d, length, up):
    if up:
        perm = [(c, c + d) for c in range(length - d)]
    else:
        perm = [(c, c - d) for c in range(d, length)]
    return lax.ppermute(x, axis, perm)


def suffix_pipeline(own, axis, n_chunks):
    length, index = (lax.axis_size(axis), lax.axis_index(axis))
    rows, cols = own.shape
    height = rows // n_chunks
    chunks = own.reshape(n_chunks, height, cols)
    pad = jnp.zeros((length - 1, height, cols), own.dtype)
    padded = jnp.concatenate((pad, chunks, pad), axis=0)
    steps = n_chunks + length - 1
    ordered = lax.dynamic_slice_in_dim(padded, index, steps, axis=0)
    perm = [(i, i - 1) for i in range(1, length)]
    recv = jnp.zeros((height, cols), jnp.bfloat16)
    done = []
    for tau in range(steps):
        acc = (chunks[0] if tau == 0 else ordered[tau]) + recv.astype(jnp.float32)
        done.append(acc)
        if tau < steps - 1:
            recv = lax.ppermute(acc.astype(jnp.bfloat16), axis, perm)
    stacked = jnp.stack(done, axis=0)
    mine = lax.dynamic_slice_in_dim(stacked, length - 1 - index, n_chunks, axis=0)
    return mine.reshape(rows, cols)


def attention_terms(q3, g3, kv_blocks, lower, upper, kv_local, head_dim, scaling):
    tok_rows = q3.shape[1]
    group = q3.shape[0] // kv_local
    n_blocks = len(kv_blocks)
    seq_rows = tok_rows * n_blocks
    kv_cols = kv_local * head_dim
    nt = (((1,), (1,)), ((), ()))

    def kernel(*refs):
        q_ref, g_ref = refs[0], refs[1]
        kv_refs = refs[2 : 2 + n_blocks]
        lo_ref, hi_ref, own_ref = refs[2 + n_blocks : 5 + n_blocks]
        send_refs = refs[5 + n_blocks :]
        rows = lax.broadcasted_iota(jnp.int32, (seq_rows, tok_rows), 1)
        allowed = (lo_ref[...] <= rows) & (rows <= hi_ref[...])
        for k in range(kv_local):
            kcols = slice(k * head_dim, (k + 1) * head_dim)
            vcols = slice(kv_cols + k * head_dim, kv_cols + (k + 1) * head_dim)
            key = jnp.concatenate([r[:, kcols] for r in kv_refs], axis=0)
            val = jnp.concatenate([r[:, vcols] for r in kv_refs], axis=0)
            dk = jnp.zeros((seq_rows, head_dim), jnp.float32)
            dv = jnp.zeros((seq_rows, head_dim), jnp.float32)
            for j in range(group):
                h = k * group + j
                q = q_ref[h]
                gr = g_ref[h]
                s = lax.dot_general(key, q, nt, preferred_element_type=jnp.float32) * scaling
                masked = jnp.where(allowed, s, -1e30)
                top = jnp.max(masked, axis=0, keepdims=True)
                e = jnp.exp(masked - top)
                tot = jnp.sum(e, axis=0, keepdims=True)
                p = e * (1.0 / tot)
                pb = p.astype(jnp.bfloat16)
                dp = lax.dot_general(val, gr, nt, preferred_element_type=jnp.float32)
                rd = jnp.sum(pb.astype(jnp.float32) * dp, axis=0, keepdims=True)
                ds = (p * (dp - rd)).astype(jnp.bfloat16)
                dv = dv + jnp.dot(pb, gr, preferred_element_type=jnp.float32)
                dk = dk + jnp.dot(ds, q, preferred_element_type=jnp.float32)
            dk = dk * scaling
            own_ref[:, kcols] = dk[:tok_rows]
            own_ref[:, vcols] = dv[:tok_rows]
            for p, send_ref in enumerate(send_refs, start=1):
                send_ref[:, kcols] = dk[p * tok_rows : (p + 1) * tok_rows].astype(jnp.bfloat16)
                send_ref[:, vcols] = dv[p * tok_rows : (p + 1) * tok_rows].astype(jnp.bfloat16)

    return pl.pallas_call(
        kernel,
        out_shape=(jax.ShapeDtypeStruct((tok_rows, 2 * kv_cols), jnp.float32),)
        + tuple(
            jax.ShapeDtypeStruct((tok_rows, 2 * kv_cols), jnp.bfloat16) for _ in range(n_blocks - 1)
        ),
    )(q3, g3, *kv_blocks, lower, upper)


def per_device(inputs, query, grad_out, w_key, w_value, keep_mask):
    tok_rows = inputs.shape[1]
    local_heads = query.shape[2]
    head_dim = query.shape[3]
    kv_cols = w_key.shape[2]
    kv_local = kv_cols // head_dim
    group_size = local_heads // kv_local
    scaling = 1.0 / math.sqrt(head_dim)
    ctx_len = lax.axis_size("ctx")
    ctx_index = lax.axis_index("ctx")
    tokens = inputs[0]
    key_rows = jnp.dot(tokens, w_key[0], preferred_element_type=jnp.float32).astype(jnp.bfloat16)
    value_rows = jnp.dot(tokens, w_value[0], preferred_element_type=jnp.float32).astype(
        jnp.bfloat16
    )
    kv_own = jnp.concatenate((key_rows, value_rows), axis=1)
    later = {d: shifted(kv_own, "ctx", d, ctx_len, True) for d in range(ctx_len - 1, 0, -1)}
    blocks = [kv_own] + [later[d] for d in range(1, ctx_len)]
    seq_rows = tok_rows * ctx_len
    first_row = ctx_index * tok_rows
    blk = jnp.arange(ctx_len, dtype=jnp.int32)
    col_pos = (
        (ctx_index - blk)[:, None] * tok_rows + jnp.arange(tok_rows, dtype=jnp.int32)[None, :]
    ).reshape(seq_rows, 1)
    keep_blocks = keep_mask.reshape(ctx_len, tok_rows)
    kept = jnp.concatenate(
        [
            lax.dynamic_index_in_dim(keep_blocks, jnp.maximum(ctx_index - p, 0), 0, keepdims=False)
            for p in range(ctx_len)
        ],
        axis=0,
    ).reshape(seq_rows, 1)
    never = jnp.iinfo(jnp.int32).max
    lower = jnp.where(col_pos >= 0, col_pos - first_row, never)
    upper = jnp.where(kept == 1, never, col_pos - first_row)
    q3 = jnp.transpose(query[0], (1, 0, 2))
    g3 = jnp.transpose(grad_out[0], (1, 0, 2))
    kv_grad, *parts = attention_terms(q3, g3, blocks, lower, upper, kv_local, head_dim, scaling)
    for d in range(1, ctx_len):
        part = parts[d - 1]
        kv_grad = kv_grad + shifted(part, "ctx", d, ctx_len, False).astype(jnp.float32)
    grad_key = kv_grad[:, :kv_cols].astype(jnp.bfloat16)
    grad_value = kv_grad[:, kv_cols:].astype(jnp.bfloat16)
    contract = (((1,), (1,)), ((), ()))
    head_len = lax.axis_size("head")
    head_index = lax.axis_index("head")
    out_cols = w_key.shape[1] // head_len

    def partial_for(b):
        start = b * out_cols
        wk = lax.dynamic_slice_in_dim(w_key[0], start, out_cols, axis=0)
        wv = lax.dynamic_slice_in_dim(w_value[0], start, out_cols, axis=0)
        part = lax.dot_general(grad_key, wk, contract, preferred_element_type=jnp.float32)
        return part + lax.dot_general(grad_value, wv, contract, preferred_element_type=jnp.float32)

    received = []
    for d in range(1, head_len):
        target = lax.rem(head_index + d, head_len)
        send = partial_for(target).astype(jnp.bfloat16)
        perm = [(h, (h + d) % head_len) for h in range(head_len)]
        received.append(lax.ppermute(send, "head", perm))
    reduced = partial_for(head_index)
    for got in received:
        reduced = reduced + got.astype(jnp.float32)
    result = suffix_pipeline(reduced, "segment", CHAIN_CHUNKS)
    return result[None]


def solution(mesh):
    return jax.shard_map(
        per_device,
        mesh=mesh,
        in_specs=(
            P("segment", "ctx", None),
            P("segment", "ctx", "head", None),
            P("segment", "ctx", "head", None),
            P("segment", None, "head"),
            P("segment", None, "head"),
            P(),
        ),
        out_specs=P("segment", "ctx", "head"),
        check_vma=False,
    )
```

```python
import math

import jax
import jax.numpy as jnp
from jax import lax
from jax.experimental import pallas as pl
from jax.sharding import PartitionSpec as P


CHAIN_CHUNKS = 2


def shifted(x, axis, d, length, up):
    if up:
        perm = [(c, c + d) for c in range(length - d)]
    else:
        perm = [(c, c - d) for c in range(d, length)]
    return lax.ppermute(x, axis, perm)


def suffix_pipeline(own, axis, n_chunks):
    length, index = (lax.axis_size(axis), lax.axis_index(axis))
    rows, cols = own.shape
    height = rows // n_chunks
    chunks = own.reshape(n_chunks, height, cols)
    pad = jnp.zeros((length - 1, height, cols), own.dtype)
    padded = jnp.concatenate((pad, chunks, pad), axis=0)
    steps = n_chunks + length - 1
    ordered = lax.dynamic_slice_in_dim(padded, index, steps, axis=0)
    perm = [(i, i - 1) for i in range(1, length)]
    recv = jnp.zeros((height, cols), jnp.bfloat16)
    done = []
    for tau in range(steps):
        acc = (chunks[0] if tau == 0 else ordered[tau]) + recv.astype(jnp.float32)
        done.append(acc)
        if tau < steps - 1:
            recv = lax.ppermute(acc.astype(jnp.bfloat16), axis, perm)
    mine = [
        lax.dynamic_index_in_dim(
            jnp.stack(done[k : k + length], axis=0), length - 1 - index, 0, keepdims=False
        )
        for k in range(n_chunks)
    ]
    return jnp.concatenate(mine, axis=0)


def attention_terms(q3, g3, kv_blocks, lower, upper, kv_local, head_dim, scaling):
    tok_rows = q3.shape[1]
    group = q3.shape[0] // kv_local
    n_blocks = len(kv_blocks)
    seq_rows = tok_rows * n_blocks
    kv_cols = kv_local * head_dim
    nt = (((1,), (1,)), ((), ()))

    def kernel(*refs):
        q_ref, g_ref = refs[0], refs[1]
        kv_refs = refs[2 : 2 + n_blocks]
        lo_ref, hi_ref, own_ref = refs[2 + n_blocks : 5 + n_blocks]
        send_refs = refs[5 + n_blocks :]
        rows = lax.broadcasted_iota(jnp.int32, (seq_rows, tok_rows), 1)
        allowed = (lo_ref[...] <= rows) & (rows <= hi_ref[...])
        for k in range(kv_local):
            kcols = slice(k * head_dim, (k + 1) * head_dim)
            vcols = slice(kv_cols + k * head_dim, kv_cols + (k + 1) * head_dim)
            key = jnp.concatenate([r[:, kcols] for r in kv_refs], axis=0)
            val = jnp.concatenate([r[:, vcols] for r in kv_refs], axis=0)
            dk = jnp.zeros((seq_rows, head_dim), jnp.float32)
            dv = jnp.zeros((seq_rows, head_dim), jnp.float32)
            for j in range(group):
                h = k * group + j
                q = q_ref[h]
                gr = g_ref[h]
                s = lax.dot_general(key, q, nt, preferred_element_type=jnp.float32) * scaling
                masked = jnp.where(allowed, s, -1e30)
                top = jnp.max(masked, axis=0, keepdims=True)
                e = jnp.exp(masked - top)
                tot = jnp.sum(e, axis=0, keepdims=True)
                p = e * (1.0 / tot)
                pb = p.astype(jnp.bfloat16)
                dp = lax.dot_general(val, gr, nt, preferred_element_type=jnp.float32)
                rd = jnp.sum(pb.astype(jnp.float32) * dp, axis=0, keepdims=True)
                ds = (p * (dp - rd)).astype(jnp.bfloat16)
                dv = dv + jnp.dot(pb, gr, preferred_element_type=jnp.float32)
                dk = dk + jnp.dot(ds, q, preferred_element_type=jnp.float32)
            dk = dk * scaling
            own_ref[:, kcols] = dk[:tok_rows]
            own_ref[:, vcols] = dv[:tok_rows]
            for p, send_ref in enumerate(send_refs, start=1):
                send_ref[:, kcols] = dk[p * tok_rows : (p + 1) * tok_rows].astype(jnp.bfloat16)
                send_ref[:, vcols] = dv[p * tok_rows : (p + 1) * tok_rows].astype(jnp.bfloat16)

    return pl.pallas_call(
        kernel,
        out_shape=(jax.ShapeDtypeStruct((tok_rows, 2 * kv_cols), jnp.float32),)
        + tuple(
            jax.ShapeDtypeStruct((tok_rows, 2 * kv_cols), jnp.bfloat16) for _ in range(n_blocks - 1)
        ),
    )(q3, g3, *kv_blocks, lower, upper)


def per_device(inputs, query, grad_out, w_key, w_value, keep_mask):
    tok_rows = inputs.shape[1]
    local_heads = query.shape[2]
    head_dim = query.shape[3]
    kv_cols = w_key.shape[2]
    kv_local = kv_cols // head_dim
    group_size = local_heads // kv_local
    scaling = 1.0 / math.sqrt(head_dim)
    ctx_len = lax.axis_size("ctx")
    ctx_index = lax.axis_index("ctx")
    tokens = inputs[0]
    key_rows = jnp.dot(tokens, w_key[0], preferred_element_type=jnp.float32).astype(jnp.bfloat16)
    value_rows = jnp.dot(tokens, w_value[0], preferred_element_type=jnp.float32).astype(
        jnp.bfloat16
    )
    kv_own = jnp.concatenate((key_rows, value_rows), axis=1)
    later = {d: shifted(kv_own, "ctx", d, ctx_len, True) for d in range(ctx_len - 1, 0, -1)}
    blocks = [kv_own] + [later[d] for d in range(1, ctx_len)]
    seq_rows = tok_rows * ctx_len
    first_row = ctx_index * tok_rows
    blk = jnp.arange(ctx_len, dtype=jnp.int32)
    col_pos = (
        (ctx_index - blk)[:, None] * tok_rows + jnp.arange(tok_rows, dtype=jnp.int32)[None, :]
    ).reshape(seq_rows, 1)
    keep_blocks = keep_mask.reshape(ctx_len, tok_rows)
    kept = jnp.concatenate(
        [
            lax.dynamic_index_in_dim(keep_blocks, jnp.maximum(ctx_index - p, 0), 0, keepdims=False)
            for p in range(ctx_len)
        ],
        axis=0,
    ).reshape(seq_rows, 1)
    never = jnp.iinfo(jnp.int32).max
    lower = jnp.where(col_pos >= 0, col_pos - first_row, never)
    upper = jnp.where(kept == 1, never, col_pos - first_row)
    q3 = jnp.transpose(query[0], (1, 0, 2))
    g3 = jnp.transpose(grad_out[0], (1, 0, 2))
    kv_grad, *parts = attention_terms(q3, g3, blocks, lower, upper, kv_local, head_dim, scaling)
    for d in range(1, ctx_len):
        part = parts[d - 1]
        kv_grad = kv_grad + shifted(part, "ctx", d, ctx_len, False).astype(jnp.float32)
    grad_key = kv_grad[:, :kv_cols].astype(jnp.bfloat16)
    grad_value = kv_grad[:, kv_cols:].astype(jnp.bfloat16)
    contract = (((1,), (1,)), ((), ()))
    head_len = lax.axis_size("head")
    head_index = lax.axis_index("head")
    out_cols = w_key.shape[1] // head_len

    def partial_for(b):
        start = b * out_cols
        wk = lax.dynamic_slice_in_dim(w_key[0], start, out_cols, axis=0)
        wv = lax.dynamic_slice_in_dim(w_value[0], start, out_cols, axis=0)
        part = lax.dot_general(grad_key, wk, contract, preferred_element_type=jnp.float32)
        return part + lax.dot_general(grad_value, wv, contract, preferred_element_type=jnp.float32)

    received = []
    for d in range(1, head_len):
        target = lax.rem(head_index + d, head_len)
        send = partial_for(target).astype(jnp.bfloat16)
        perm = [(h, (h + d) % head_len) for h in range(head_len)]
        received.append(lax.ppermute(send, "head", perm))
    reduced = partial_for(head_index)
    for got in received:
        reduced = reduced + got.astype(jnp.float32)
    result = suffix_pipeline(reduced, "segment", CHAIN_CHUNKS)
    return result[None]


def solution(mesh):
    return jax.shard_map(
        per_device,
        mesh=mesh,
        in_specs=(
            P("segment", "ctx", None),
            P("segment", "ctx", "head", None),
            P("segment", "ctx", "head", None),
            P("segment", None, "head"),
            P("segment", None, "head"),
            P(),
        ),
        out_specs=P("segment", "ctx", "head"),
        check_vma=False,
    )
```
